256 devices in a mesh: tile: 16 (over y, x), query: 2 (over core), dp: 8 (over z).
Axes of the slice: x: 4, y: 4, z: 8, core: 2. Of those that a mesh axis runs over, the one named last changes fastest.
Arguments:
- features: bfloat16 [8, 131072, 256], P('dp', ('tile', 'query')), may hold values from -6 to 6
- queries: bfloat16 [8, 256, 256], P('dp', ('tile', 'query')), may hold values from -6 to 6
- out_grad: bfloat16 [8, 256, 256], P('dp', ('tile', 'query')), may hold values from -48 to 48
- value_weight: bfloat16 [256, 256], replicated, may hold values from -0.375 to 0.375
- attn_weight: bfloat16 [256, 128], replicated, may hold values from -0.375 to 0.375
- out_weight: bfloat16 [256, 256], replicated, may hold values from -0.375 to 0.375
- slot_point: int32 [8, 65536], P('dp', ('tile', 'query')), may hold values from 0 to 32767, as said below
- slot_rows: int32 [8, 4, 65536], P('dp', None, ('tile', 'query')), may hold values from 0 to 4095, as said below
- slot_bilinear: float32 [8, 4, 65536], P('dp', None, ('tile', 'query')), may hold values from 0 to 1, as said below
- slot_count: int32 [8, 32], P('dp', ('tile', 'query')), may hold values from 1 to 2048, as said below
Outputs:
- feature_grad: bfloat16 [8, 131072, 256], P('dp', ('tile', 'query'))
- query_grad: bfloat16 [8, 256, 256], P('dp', ('tile', 'query'))
- value_weight_grad: float32 [256, 256], replicated
- attn_weight_grad: float32 [256, 128], replicated
- out_weight_grad: float32 [256, 256], replicated
The draws below stay inside these ranges and needn't reach their ends.
Inputs may be any that keep to these rules, and one draw needn't show every extreme that they name: `slot_count`: per page one owner has exactly 2048 live slots; the counts of a page sum to 32768. `slot_point`: the live slots of a page name every sample point exactly once, point m = q * 128 + head * 4 * 4 + level * 4 + point; slots that are not live hold arbitrary point numbers. `slot_rows`: the corners of a slot are rows r, r + 1, r + 64, r + 65 of the owner's tokens laid out in lines of 64. `slot_bilinear`: the four weights of a slot sum to one.
All inputs are finite; a program needn't handle non-finite values.
Results may differ from the reference program's by a relative error of at most 0.0064.
Values may be sent and summed in bfloat16 or wider, within the bound.
No kernel may reach another device: no remote copies, remote signals or barrier semaphores. Data moves between devices by JAX's collectives and lax.ppermute only.
A program may use at most 128 MiB of HBM per device.

```python
import jax
import jax.numpy as jnp
from jax import lax

D = 256
HEADS = 8
LEVELS = 4
POINTS = 4
TILE_W = 64
TOK_DEV = 4096
OWNERS = 32
PAGES = 8
QUERIES = 256
TOKENS = 131072
ATT = 128
CAP = 2048
SLOTS = 65536


def page_counts(page_key):
    all_points = QUERIES * HEADS * LEVELS * POINTS
    remaining = all_points - CAP
    first_key, second_key = jax.random.split(page_key)
    weights = jax.random.randint(first_key, (OWNERS,), 2, 4)
    busiest = jax.random.randint(second_key, (), 0, OWNERS)
    is_busiest = jnp.arange(OWNERS) == busiest
    weights = jnp.where(is_busiest, 0, weights)
    shares = remaining * weights // jnp.sum(weights)
    leftover = remaining - jnp.sum(shares)
    ranked = jnp.cumsum(jnp.where(is_busiest, 0, 1)) - 1
    shares = shares + jnp.where(jnp.logical_and(jnp.logical_not(is_busiest), ranked < leftover), 1, 0)
    return jnp.where(is_busiest, CAP, shares).astype(jnp.int32)


def page_points(page_key):
    all_points = QUERIES * HEADS * LEVELS * POINTS
    counts = page_counts(jax.random.fold_in(page_key, 1))
    shuffled = jax.random.permutation(jax.random.fold_in(page_key, 2), all_points).astype(jnp.int32)
    starts = jnp.cumsum(counts) - counts
    slot_ids = jnp.arange(OWNERS * CAP)
    owner_index = slot_ids // CAP
    within = slot_ids % CAP
    position = jnp.minimum(starts[owner_index] + within, all_points - 1)
    filler = jax.random.randint(jax.random.fold_in(page_key, 3), (OWNERS * CAP,), 0, all_points)
    return jnp.where(within < counts[owner_index], shuffled[position], filler).astype(jnp.int32)


def page_key_list(key):
    return jax.random.split(jax.random.fold_in(key, 5), PAGES)


def count_of_page(page_key):
    return page_counts(jax.random.fold_in(page_key, 1))


def draw_slot_count(key, part):
    return jax.vmap(count_of_page)(page_key_list(key))


def draw_slot_point(key, part):
    return jax.vmap(page_points)(page_key_list(key))


def draw_slot_rows(key, part):
    first_key, second_key = jax.random.split(jax.random.fold_in(key, 31))
    grid_lines = TOK_DEV // TILE_W
    row_y = jax.random.randint(first_key, (PAGES, SLOTS), 0, grid_lines - 1)
    row_x = jax.random.randint(second_key, (PAGES, SLOTS), 0, TILE_W - 1)
    base_row = row_y * TILE_W + row_x
    return jnp.stack([base_row, base_row + 1, base_row + TILE_W, base_row + TILE_W + 1], axis=1).astype(jnp.int32)


def draw_slot_bilinear(key, part):
    first_key, second_key = jax.random.split(jax.random.fold_in(key, 41))
    frac_x = jax.random.uniform(first_key, (PAGES, SLOTS), jnp.float32)
    frac_y = jax.random.uniform(second_key, (PAGES, SLOTS), jnp.float32)
    return jnp.stack([(1.0 - frac_x) * (1.0 - frac_y), frac_x * (1.0 - frac_y), (1.0 - frac_x) * frac_y, frac_x * frac_y], axis=1).astype(jnp.float32)


def steps_of(rng, extent, pieces, smallest, high):
    factor_of = 1.0
    for dim, shards_of in pieces:
        steps = jax.random.uniform(jax.random.fold_in(jax.random.fold_in(rng, 6), dim), (shards_of,), jnp.float32, smallest / len(pieces), high / len(pieces))
        factor_of = factor_of * jnp.repeat(jnp.exp(steps), extent[dim] // shards_of).reshape((-1,) + (1,) * (len(extent) - 1 - dim))
    return factor_of


def scatter_about(rng, shape, width, limit, pieces=(), kind=jnp.bfloat16):
    level = steps_of(rng, shape, pieces, -0.22, 0.18) if pieces else 1.0
    values = jax.random.normal(rng, shape, jnp.float32) * width * level
    return jnp.minimum(jnp.maximum(values, -limit), limit).astype(kind)


def setup_inputs(seed: int = 0) -> dict:
    keys = jax.random.split(jax.random.key(seed), 11)
    return {
        "features": scatter_about(keys[0], (PAGES, TOKENS, D), 1.0, 6.0, ((0, 8), (1, 32))),
        "queries": scatter_about(keys[1], (PAGES, QUERIES, D), 1.0, 6.0, ((0, 8), (1, 32))),
        "out_grad": scatter_about(keys[2], (PAGES, QUERIES, D), 8.0, 48.0, ((0, 8), (1, 32))),
        "value_weight": scatter_about(keys[3], (D, D), D ** -0.5, 0.375),
        "attn_weight": scatter_about(keys[4], (D, ATT), D ** -0.5, 0.375),
        "out_weight": scatter_about(keys[5], (D, D), D ** -0.5, 0.375),
        "slot_point": draw_slot_point(jax.random.fold_in(keys[10], 71), 0),
        "slot_rows": draw_slot_rows(jax.random.fold_in(keys[10], 71), 0),
        "slot_bilinear": draw_slot_bilinear(jax.random.fold_in(keys[10], 71), 0),
        "slot_count": draw_slot_count(jax.random.fold_in(keys[10], 71), 0),
    }


def over_rows(left, right):
    return lax.dot_general(left, right, (((0,), (0,)), ((), ())), preferred_element_type=jnp.float32)


def over_rows_exact(left, right):
    return lax.dot_general(left, right, (((0,), (0,)), ((), ())), precision=lax.Precision.HIGHEST, preferred_element_type=jnp.float32)


def times_transpose(left, right):
    return lax.dot_general(left, right, (((1,), (1,)), ((), ())), preferred_element_type=jnp.float32)


def reference(features, queries, out_grad, value_weight, attn_weight, out_weight, slot_point, slot_rows, slot_bilinear, slot_count):
    per_head = LEVELS * POINTS
    head_width = D // HEADS
    grad_scale = float(PAGES * QUERIES) ** -0.5

    def one_page(page_args):
        page_feats, page_queries, page_out, points, token_rows, bilinear_all, counts = page_args
        projected = jnp.dot(page_feats, value_weight, preferred_element_type=jnp.float32).astype(jnp.bfloat16)
        exponent = jnp.exp(jnp.dot(page_queries, attn_weight, preferred_element_type=jnp.float32)).reshape(QUERIES, HEADS, per_head)
        attention = (exponent / jnp.sum(exponent, axis=2, keepdims=True)).reshape(QUERIES, ATT)
        attn_rounded = attention.astype(jnp.bfloat16)
        sample_grad = times_transpose(page_out, out_weight).astype(jnp.bfloat16)
        slot_ids = jnp.arange(SLOTS, dtype=jnp.int32)
        owner_index = (slot_ids // CAP).astype(jnp.int32)
        alive_slot = (slot_ids % CAP) < counts[owner_index]
        query_index = (points // ATT).astype(jnp.int32)
        attn_column = (points % ATT).astype(jnp.int32)
        head_index = attn_column // per_head
        weight = jnp.where(alive_slot, attn_rounded[query_index, attn_column].astype(jnp.float32), jnp.zeros((), jnp.float32))
        head_mask = (jnp.arange(D, dtype=jnp.int32)[None, :] // head_width) == head_index[:, None]
        slot_grad = jnp.where(head_mask, sample_grad[query_index], jnp.zeros((), jnp.bfloat16)).astype(jnp.float32)
        mixed_rows = jnp.zeros((SLOTS, D), jnp.float32)
        corner_dots = jnp.zeros((SLOTS,), jnp.float32)
        value_grad = jnp.zeros((TOKENS, D), jnp.float32)
        for corner in range(4):
            token_row = (token_rows[corner] + owner_index * TOK_DEV).astype(jnp.int32)
            bilinear = bilinear_all[corner]
            picked = projected[token_row].astype(jnp.float32)
            mixed_rows = mixed_rows + bilinear[:, None] * picked
            corner_dots = corner_dots + bilinear * jnp.sum(picked * slot_grad, axis=1)
            value_grad = value_grad.at[token_row].add((weight * bilinear)[:, None] * slot_grad)
        sampled = jnp.zeros((QUERIES, D), jnp.float32).at[query_index].add(jnp.where(head_mask, weight[:, None] * mixed_rows, jnp.zeros((), jnp.float32)))
        attn_grad = jnp.zeros((QUERIES, ATT), jnp.float32).at[query_index, attn_column].add(jnp.where(alive_slot, corner_dots, jnp.zeros((), jnp.float32)))
        attn_three = attention.reshape(QUERIES, HEADS, per_head)
        grad_three = attn_grad.reshape(QUERIES, HEADS, per_head)
        logit_grad = (attn_three * (grad_three - jnp.sum(attn_three * grad_three, axis=2, keepdims=True))).reshape(QUERIES, ATT).astype(jnp.bfloat16)
        query_grad = times_transpose(logit_grad, attn_weight).astype(jnp.bfloat16)
        value_rounded = value_grad.astype(jnp.bfloat16)
        feature_grad = times_transpose(value_rounded, value_weight).astype(jnp.bfloat16)
        value_term = over_rows(page_feats, value_rounded)
        attn_term = over_rows(page_queries, logit_grad)
        out_term = over_rows_exact(sampled, page_out.astype(jnp.float32))
        return feature_grad, query_grad, value_term, attn_term, out_term

    results = lax.map(one_page, (features, queries, out_grad, slot_point, slot_rows, slot_bilinear, slot_count))
    feature_grad, query_grad, value_terms, attn_terms, out_terms = results
    return (feature_grad, query_grad, jnp.sum(value_terms, axis=0) * grad_scale, jnp.sum(attn_terms, axis=0) * grad_scale, jnp.sum(out_terms, axis=0) * grad_scale)
```

```python
import jax
import jax.numpy as jnp
from jax import lax
from jax.sharding import PartitionSpec as P

HEADS = 8
TILE_W = 64


def over_rows(left, right):
    return lax.dot_general(
        left, right, (((0,), (0,)), ((), ())), preferred_element_type=jnp.float32
    )


def over_rows_exact(left, right):
    return lax.dot_general(
        left,
        right,
        (((0,), (0,)), ((), ())),
        precision=lax.Precision.HIGHEST,
        preferred_element_type=jnp.float32,
    )


def times_transpose(left, right):
    return lax.dot_general(
        left, right, (((1,), (1,)), ((), ())), preferred_element_type=jnp.float32
    )


def gather_rows(block, axes):
    count = lax.axis_size(axes)
    copies = jnp.broadcast_to(block[None], (count,) + block.shape)
    gathered = lax.all_to_all(copies, axes, 0, 0, tiled=True)
    return gathered.reshape((count * block.shape[0],) + block.shape[1:])


def scatter_sum_rows(block, axes):
    count = lax.axis_size(axes)
    pieces = block.reshape((count, block.shape[0] // count) + block.shape[1:])
    return jnp.sum(lax.all_to_all(pieces, axes, 0, 0, tiled=True), axis=0)


def sum_everywhere(block, stages):
    for axis in stages:
        block = scatter_sum_rows(block, axis)
    for axis in reversed(stages):
        block = gather_rows(block, axis)
    return block


def shift_down(block, offset):
    return jnp.concatenate(
        [jnp.zeros((offset, block.shape[1]), block.dtype), block[: block.shape[0] - offset]], axis=0
    )


def local(
    features,
    queries,
    out_grad,
    value_weight,
    attn_weight,
    out_weight,
    slot_point,
    slot_rows,
    slot_bilinear,
    slot_count,
):
    owners = lax.axis_size(("tile", "query"))
    page_count = lax.axis_size("dp")
    local_queries = queries.shape[1]
    all_queries = local_queries * owners
    grad_scale = float(page_count * all_queries) ** (-0.5)
    width = features.shape[2]
    att_width = attn_weight.shape[1]
    per_head = att_width // HEADS
    head_width = width // HEADS
    exponent = jnp.exp(
        jnp.dot(queries[0], attn_weight, preferred_element_type=jnp.float32)
    ).reshape(local_queries, HEADS, per_head)
    attention = (exponent / jnp.sum(exponent, axis=2, keepdims=True)).reshape(
        local_queries, att_width
    )
    attn_rounded = attention.astype(jnp.bfloat16)
    sample_grad = times_transpose(out_grad[0], out_weight).astype(jnp.bfloat16)
    every_both = gather_rows(
        jnp.concatenate([sample_grad, attn_rounded], axis=1), ("tile", "query")
    )
    every_grad = every_both[:, :width]
    every_attn = every_both[:, width:]
    projected = jnp.dot(features[0], value_weight, preferred_element_type=jnp.float32).astype(
        jnp.bfloat16
    )
    token_count = projected.shape[0]
    capacity = slot_point.shape[1]
    points = slot_point[0]
    alive_slot = jnp.arange(capacity, dtype=jnp.int32) < slot_count[0, 0]
    query_index = points // att_width
    attn_column = points % att_width
    head_index = attn_column // per_head
    query_match = query_index[:, None] == jnp.arange(all_queries, dtype=jnp.int32)[None, :]
    query_onehot = query_match.astype(jnp.bfloat16)
    column_match = attn_column[:, None] == jnp.arange(att_width, dtype=jnp.int32)[None, :]
    attn_rows = jnp.dot(query_onehot, every_attn, preferred_element_type=jnp.float32)
    picked_attn = jnp.sum(jnp.where(column_match, attn_rows, jnp.zeros((), jnp.float32)), axis=1)
    weight = jnp.where(alive_slot, picked_attn, jnp.zeros((), jnp.float32))
    head_mask = jnp.arange(width, dtype=jnp.int32)[None, :] // head_width == head_index[:, None]
    grad_rows = jnp.dot(query_onehot, every_grad, preferred_element_type=jnp.float32)
    slot_grad = jnp.where(head_mask, grad_rows, jnp.zeros((), jnp.float32))
    offsets = (0, 1, TILE_W, TILE_W + 1)
    padded = jnp.concatenate([projected, jnp.zeros((TILE_W + 1, width), jnp.bfloat16)], axis=0)
    corner_table = jnp.concatenate(
        [padded[offset : offset + token_count] for offset in offsets], axis=1
    )
    base_row = slot_rows[0, 0]
    picked_all = corner_table[base_row].astype(jnp.float32)
    mixed_rows = jnp.zeros((capacity, width), jnp.float32)
    corner_dots = jnp.zeros((capacity,), jnp.float32)
    contributions = []
    for corner in range(4):
        bilinear = slot_bilinear[0, corner]
        picked = picked_all[:, corner * width : (corner + 1) * width]
        mixed_rows = mixed_rows + bilinear[:, None] * picked
        corner_dots = corner_dots + bilinear * jnp.sum(picked * slot_grad, axis=1)
        contributions.append((weight * bilinear)[:, None] * slot_grad)
    corner_sums = (
        jnp.zeros((token_count, 4 * width), jnp.float32)
        .at[base_row]
        .add(jnp.concatenate(contributions, axis=1))
    )
    value_grad = corner_sums[:, 0:width]
    for corner in range(1, 4):
        value_grad = value_grad + shift_down(
            corner_sums[:, corner * width : (corner + 1) * width], offsets[corner]
        )
    query_float = query_match.astype(jnp.float32)
    sampled_part = over_rows_exact(
        query_float, jnp.where(head_mask, weight[:, None] * mixed_rows, jnp.zeros((), jnp.float32))
    )
    dots_table = jnp.where(
        jnp.logical_and(column_match, alive_slot[:, None]),
        corner_dots[:, None],
        jnp.zeros((), jnp.float32),
    )
    attn_part = over_rows_exact(query_float, dots_table)
    shares = scatter_sum_rows(
        jnp.concatenate([sampled_part, attn_part], axis=1), ("tile", "query")
    )
    sampled_share = shares[:, :width]
    attn_grad = shares[:, width:]
    out_term = over_rows_exact(sampled_share, out_grad[0].astype(jnp.float32))
    attn_three = attention.reshape(local_queries, HEADS, per_head)
    grad_three = attn_grad.reshape(local_queries, HEADS, per_head)
    logit_grad = (
        (attn_three * (grad_three - jnp.sum(attn_three * grad_three, axis=2, keepdims=True)))
        .reshape(local_queries, att_width)
        .astype(jnp.bfloat16)
    )
    query_grad = times_transpose(logit_grad, attn_weight).astype(jnp.bfloat16)
    value_rounded = value_grad.astype(jnp.bfloat16)
    feature_grad = times_transpose(value_rounded, value_weight).astype(jnp.bfloat16)
    value_term = over_rows(features[0], value_rounded)
    attn_term = over_rows(queries[0], logit_grad)
    summed = sum_everywhere(
        jnp.concatenate([value_term, attn_term, out_term], axis=1), ("query", "tile", "dp")
    )
    return (
        feature_grad[None],
        query_grad[None],
        summed[:, :width] * grad_scale,
        summed[:, width : width + att_width] * grad_scale,
        summed[:, width + att_width :] * grad_scale,
    )


def solution(mesh):
    in_specs = (
        P("dp", ("tile", "query"), None),
        P("dp", ("tile", "query"), None),
        P("dp", ("tile", "query"), None),
        P(),
        P(),
        P(),
        P("dp", ("tile", "query")),
        P("dp", None, ("tile", "query")),
        P("dp", None, ("tile", "query")),
        P("dp", ("tile", "query")),
    )
    out_specs = (P("dp", ("tile", "query"), None), P("dp", ("tile", "query"), None), P(), P(), P())
    return jax.shard_map(local, mesh=mesh, in_specs=in_specs, out_specs=out_specs, check_vma=False)
```

```python
import jax
import jax.numpy as jnp
from jax import lax
from jax.sharding import PartitionSpec as P

HEADS = 8
TILE_W = 64


def over_rows(left, right):
    return lax.dot_general(
        left, right, (((0,), (0,)), ((), ())), preferred_element_type=jnp.float32
    )


def over_rows_exact(left, right):
    return lax.dot_general(
        left,
        right,
        (((0,), (0,)), ((), ())),
        precision=lax.Precision.HIGHEST,
        preferred_element_type=jnp.float32,
    )


def times_transpose(left, right):
    return lax.dot_general(
        left, right, (((1,), (1,)), ((), ())), preferred_element_type=jnp.float32
    )


def gather_rows(block, axes):
    count = lax.axis_size(axes)
    copies = jnp.broadcast_to(block[None], (count,) + block.shape)
    gathered = lax.all_to_all(copies, axes, 0, 0, tiled=True)
    return gathered.reshape((count * block.shape[0],) + block.shape[1:])


def scatter_sum_rows(block, axes):
    count = lax.axis_size(axes)
    pieces = block.reshape((count, block.shape[0] // count) + block.shape[1:])
    return jnp.sum(lax.all_to_all(pieces, axes, 0, 0, tiled=True), axis=0)


def sum_everywhere(block):
    block = scatter_sum_rows(block, ("tile", "query"))
    count = lax.axis_size("dp")
    copies = jnp.broadcast_to(block[None], (count,) + block.shape)
    block = jnp.sum(lax.all_to_all(copies, "dp", 0, 0, tiled=True), axis=0)
    return gather_rows(block, ("tile", "query"))

def shift_down(block, offset):
    return jnp.concatenate(
        [jnp.zeros((offset, block.shape[1]), block.dtype), block[: block.shape[0] - offset]], axis=0
    )


def local(
    features,
    queries,
    out_grad,
    value_weight,
    attn_weight,
    out_weight,
    slot_point,
    slot_rows,
    slot_bilinear,
    slot_count,
):
    owners = lax.axis_size(("tile", "query"))
    page_count = lax.axis_size("dp")
    local_queries = queries.shape[1]
    all_queries = local_queries * owners
    grad_scale = float(page_count * all_queries) ** (-0.5)
    width = features.shape[2]
    att_width = attn_weight.shape[1]
    per_head = att_width // HEADS
    head_width = width // HEADS
    exponent = jnp.exp(
        jnp.dot(queries[0], attn_weight, preferred_element_type=jnp.float32)
    ).reshape(local_queries, HEADS, per_head)
    attention = (exponent / jnp.sum(exponent, axis=2, keepdims=True)).reshape(
        local_queries, att_width
    )
    attn_rounded = attention.astype(jnp.bfloat16)
    sample_grad = times_transpose(out_grad[0], out_weight).astype(jnp.bfloat16)
    every_both = gather_rows(
        jnp.concatenate([sample_grad, attn_rounded], axis=1), ("tile", "query")
    )
    every_grad = every_both[:, :width]
    every_attn = every_both[:, width:]
    projected = jnp.dot(features[0], value_weight, preferred_element_type=jnp.float32).astype(
        jnp.bfloat16
    )
    token_count = projected.shape[0]
    capacity = slot_point.shape[1]
    points = slot_point[0]
    alive_slot = jnp.arange(capacity, dtype=jnp.int32) < slot_count[0, 0]
    query_index = points // att_width
    attn_column = points % att_width
    head_index = attn_column // per_head
    query_match = query_index[:, None] == jnp.arange(all_queries, dtype=jnp.int32)[None, :]
    query_onehot = query_match.astype(jnp.bfloat16)
    column_match = attn_column[:, None] == jnp.arange(att_width, dtype=jnp.int32)[None, :]
    attn_rows = jnp.dot(query_onehot, every_attn, preferred_element_type=jnp.float32)
    picked_attn = jnp.sum(jnp.where(column_match, attn_rows, jnp.zeros((), jnp.float32)), axis=1)
    weight = jnp.where(alive_slot, picked_attn, jnp.zeros((), jnp.float32))
    head_mask = jnp.arange(width, dtype=jnp.int32)[None, :] // head_width == head_index[:, None]
    grad_rows = jnp.dot(query_onehot, every_grad, preferred_element_type=jnp.float32)
    slot_grad = jnp.where(head_mask, grad_rows, jnp.zeros((), jnp.float32))
    offsets = (0, 1, TILE_W, TILE_W + 1)
    padded = jnp.concatenate([projected, jnp.zeros((TILE_W + 1, width), jnp.bfloat16)], axis=0)
    corner_table = jnp.concatenate(
        [padded[offset : offset + token_count] for offset in offsets], axis=1
    )
    base_row = slot_rows[0, 0]
    picked_all = corner_table[base_row].astype(jnp.float32)
    mixed_rows = jnp.zeros((capacity, width), jnp.float32)
    corner_dots = jnp.zeros((capacity,), jnp.float32)
    contributions = []
    for corner in range(4):
        bilinear = slot_bilinear[0, corner]
        picked = picked_all[:, corner * width : (corner + 1) * width]
        mixed_rows = mixed_rows + bilinear[:, None] * picked
        corner_dots = corner_dots + bilinear * jnp.sum(picked * slot_grad, axis=1)
        contributions.append((weight * bilinear)[:, None] * slot_grad)
    corner_sums = (
        jnp.zeros((token_count, 4 * width), jnp.float32)
        .at[base_row]
        .add(jnp.concatenate(contributions, axis=1))
    )
    value_grad = corner_sums[:, 0:width]
    for corner in range(1, 4):
        value_grad = value_grad + shift_down(
            corner_sums[:, corner * width : (corner + 1) * width], offsets[corner]
        )
    query_float = query_match.astype(jnp.float32)
    sampled_part = over_rows_exact(
        query_float, jnp.where(head_mask, weight[:, None] * mixed_rows, jnp.zeros((), jnp.float32))
    )
    dots_table = jnp.where(
        jnp.logical_and(column_match, alive_slot[:, None]),
        corner_dots[:, None],
        jnp.zeros((), jnp.float32),
    )
    attn_part = over_rows_exact(query_float, dots_table)
    shares = scatter_sum_rows(
        jnp.concatenate([sampled_part, attn_part], axis=1), ("tile", "query")
    )
    sampled_share = shares[:, :width]
    attn_grad = shares[:, width:]
    out_term = over_rows_exact(sampled_share, out_grad[0].astype(jnp.float32))
    attn_three = attention.reshape(local_queries, HEADS, per_head)
    grad_three = attn_grad.reshape(local_queries, HEADS, per_head)
    logit_grad = (
        (attn_three * (grad_three - jnp.sum(attn_three * grad_three, axis=2, keepdims=True)))
        .reshape(local_queries, att_width)
        .astype(jnp.bfloat16)
    )
    query_grad = times_transpose(logit_grad, attn_weight).astype(jnp.bfloat16)
    value_rounded = value_grad.astype(jnp.bfloat16)
    feature_grad = times_transpose(value_rounded, value_weight).astype(jnp.bfloat16)
    value_term = over_rows(features[0], value_rounded)
    attn_term = over_rows(queries[0], logit_grad)
    summed = sum_everywhere(jnp.concatenate([value_term, attn_term, out_term], axis=1))
    return (
        feature_grad[None],
        query_grad[None],
        summed[:, :width] * grad_scale,
        summed[:, width : width + att_width] * grad_scale,
        summed[:, width + att_width :] * grad_scale,
    )


def solution(mesh):
    in_specs = (
        P("dp", ("tile", "query"), None),
        P("dp", ("tile", "query"), None),
        P("dp", ("tile", "query"), None),
        P(),
        P(),
        P(),
        P("dp", ("tile", "query")),
        P("dp", None, ("tile", "query")),
        P("dp", None, ("tile", "query")),
        P("dp", ("tile", "query")),
    )
    out_specs = (P("dp", ("tile", "query"), None), P("dp", ("tile", "query"), None), P(), P(), P())
    return jax.shard_map(local, mesh=mesh, in_specs=in_specs, out_specs=out_specs, check_vma=False)
```

```python
import jax
import jax.numpy as jnp
from jax import lax
from jax.experimental.layout import Layout, with_layout_constraint
from jax.sharding import PartitionSpec as P

HEADS = 8
TILE_W = 64


def over_rows(left, right):
    return lax.dot_general(
        left, right, (((0,), (0,)), ((), ())), preferred_element_type=jnp.float32
    )


def over_rows_exact(left, right):
    return lax.dot_general(
        left,
        right,
        (((0,), (0,)), ((), ())),
        precision=lax.Precision.HIGHEST,
        preferred_element_type=jnp.float32,
    )


def times_transpose(left, right):
    return lax.dot_general(
        left, right, (((1,), (1,)), ((), ())), preferred_element_type=jnp.float32
    )


def gather_rows(block, axes):
    count = lax.axis_size(axes)
    copies = jnp.broadcast_to(block[None], (count,) + block.shape)
    gathered = lax.all_to_all(copies, axes, 0, 0, tiled=True)
    return gathered.reshape((count * block.shape[0],) + block.shape[1:])


def scatter_sum_rows(block, axes):
    count = lax.axis_size(axes)
    pieces = block.reshape((count, block.shape[0] // count) + block.shape[1:])
    return jnp.sum(lax.all_to_all(pieces, axes, 0, 0, tiled=True), axis=0)


def sum_everywhere(block):
    block = scatter_sum_rows(block, ("tile", "query"))
    count = lax.axis_size("dp")
    copies = jnp.broadcast_to(block[None], (count,) + block.shape)
    block = jnp.sum(lax.all_to_all(copies, "dp", 0, 0, tiled=True), axis=0)
    return gather_rows(block, ("tile", "query"))

def row_major(block):
    return with_layout_constraint(block, Layout(major_to_minor=(0, 1)))


def shift_down(block, offset):
    return jnp.concatenate(
        [jnp.zeros((offset, block.shape[1]), block.dtype), block[: block.shape[0] - offset]], axis=0
    )


def local(
    features,
    queries,
    out_grad,
    value_weight,
    attn_weight,
    out_weight,
    slot_point,
    slot_rows,
    slot_bilinear,
    slot_count,
):
    owners = lax.axis_size(("tile", "query"))
    page_count = lax.axis_size("dp")
    local_queries = queries.shape[1]
    all_queries = local_queries * owners
    grad_scale = float(page_count * all_queries) ** (-0.5)
    width = features.shape[2]
    att_width = attn_weight.shape[1]
    per_head = att_width // HEADS
    head_width = width // HEADS
    exponent = jnp.exp(
        jnp.dot(queries[0], attn_weight, preferred_element_type=jnp.float32)
    ).reshape(local_queries, HEADS, per_head)
    attention = (exponent / jnp.sum(exponent, axis=2, keepdims=True)).reshape(
        local_queries, att_width
    )
    attn_rounded = attention.astype(jnp.bfloat16)
    sample_grad = times_transpose(out_grad[0], out_weight).astype(jnp.bfloat16)
    every_both = gather_rows(
        jnp.concatenate([sample_grad, attn_rounded], axis=1), ("tile", "query")
    )
    every_grad = every_both[:, :width]
    every_attn = every_both[:, width:]
    projected = jnp.dot(features[0], value_weight, preferred_element_type=jnp.float32).astype(
        jnp.bfloat16
    )
    token_count = projected.shape[0]
    capacity = slot_point.shape[1]
    points = slot_point[0]
    alive_slot = jnp.arange(capacity, dtype=jnp.int32) < slot_count[0, 0]
    query_index = points // att_width
    attn_column = points % att_width
    head_index = attn_column // per_head
    query_match = query_index[:, None] == jnp.arange(all_queries, dtype=jnp.int32)[None, :]
    query_onehot = query_match.astype(jnp.bfloat16)
    column_match = attn_column[:, None] == jnp.arange(att_width, dtype=jnp.int32)[None, :]
    attn_rows = jnp.dot(query_onehot, every_attn, preferred_element_type=jnp.float32)
    picked_attn = jnp.sum(jnp.where(column_match, attn_rows, jnp.zeros((), jnp.float32)), axis=1)
    weight = jnp.where(alive_slot, picked_attn, jnp.zeros((), jnp.float32))
    head_mask = jnp.arange(width, dtype=jnp.int32)[None, :] // head_width == head_index[:, None]
    grad_rows = jnp.dot(query_onehot, every_grad, preferred_element_type=jnp.float32)
    slot_grad = row_major(jnp.where(head_mask, grad_rows, jnp.zeros((), jnp.float32)))
    offsets = (0, 1, TILE_W, TILE_W + 1)
    padded = jnp.concatenate([projected, jnp.zeros((TILE_W + 1, width), jnp.bfloat16)], axis=0)
    corner_table = jnp.concatenate(
        [padded[offset : offset + token_count] for offset in offsets], axis=1
    )
    base_row = slot_rows[0, 0]
    picked_all = row_major(corner_table[base_row]).astype(jnp.float32)
    mixed_rows = jnp.zeros((capacity, width), jnp.float32)
    corner_dots = jnp.zeros((capacity,), jnp.float32)
    contributions = []
    for corner in range(4):
        bilinear = slot_bilinear[0, corner]
        picked = picked_all[:, corner * width : (corner + 1) * width]
        mixed_rows = mixed_rows + bilinear[:, None] * picked
        corner_dots = corner_dots + bilinear * jnp.sum(picked * slot_grad, axis=1)
        contributions.append((weight * bilinear)[:, None] * slot_grad)
    margin = TILE_W + 1
    corner_sums = (
        jnp.zeros((token_count + margin, 4 * width), jnp.float32)
        .at[base_row + margin]
        .add(row_major(jnp.concatenate(contributions, axis=1)))
    )
    value_grad = corner_sums[margin : margin + token_count, 0:width]
    for corner in range(1, 4):
        start = margin - offsets[corner]
        value_grad = (
            value_grad
            + corner_sums[start : start + token_count, corner * width : (corner + 1) * width]
        )
    query_float = query_match.astype(jnp.float32)
    sampled_part = over_rows_exact(
        query_float, jnp.where(head_mask, weight[:, None] * mixed_rows, jnp.zeros((), jnp.float32))
    )
    dots_table = jnp.where(
        jnp.logical_and(column_match, alive_slot[:, None]),
        corner_dots[:, None],
        jnp.zeros((), jnp.float32),
    )
    attn_part = over_rows_exact(query_float, dots_table)
    shares = scatter_sum_rows(
        jnp.concatenate([sampled_part, attn_part], axis=1), ("tile", "query")
    )
    sampled_share = shares[:, :width]
    attn_grad = shares[:, width:]
    out_term = over_rows_exact(sampled_share, out_grad[0].astype(jnp.float32))
    attn_three = attention.reshape(local_queries, HEADS, per_head)
    grad_three = attn_grad.reshape(local_queries, HEADS, per_head)
    logit_grad = (
        (attn_three * (grad_three - jnp.sum(attn_three * grad_three, axis=2, keepdims=True)))
        .reshape(local_queries, att_width)
        .astype(jnp.bfloat16)
    )
    query_grad = times_transpose(logit_grad, attn_weight).astype(jnp.bfloat16)
    value_rounded = value_grad.astype(jnp.bfloat16)
    feature_grad = times_transpose(value_rounded, value_weight).astype(jnp.bfloat16)
    value_term = over_rows(features[0], value_rounded)
    attn_term = over_rows(queries[0], logit_grad)
    summed = sum_everywhere(jnp.concatenate([value_term, attn_term, out_term], axis=1))
    return (
        feature_grad[None],
        query_grad[None],
        summed[:, :width] * grad_scale,
        summed[:, width : width + att_width] * grad_scale,
        summed[:, width + att_width :] * grad_scale,
    )


def solution(mesh):
    in_specs = (
        P("dp", ("tile", "query"), None),
        P("dp", ("tile", "query"), None),
        P("dp", ("tile", "query"), None),
        P(),
        P(),
        P(),
        P("dp", ("tile", "query")),
        P("dp", None, ("tile", "query")),
        P("dp", None, ("tile", "query")),
        P("dp", ("tile", "query")),
    )
    out_specs = (P("dp", ("tile", "query"), None), P("dp", ("tile", "query"), None), P(), P(), P())
    return jax.shard_map(local, mesh=mesh, in_specs=in_specs, out_specs=out_specs, check_vma=False)
```

```python
import jax
import jax.numpy as jnp
from jax import lax
from jax.experimental.layout import Layout, with_layout_constraint
from jax.sharding import PartitionSpec as P

HEADS = 8
TILE_W = 64


def over_rows(left, right):
    return lax.dot_general(
        left, right, (((0,), (0,)), ((), ())), preferred_element_type=jnp.float32
    )


def over_rows_exact(left, right):
    return lax.dot_general(
        left,
        right,
        (((0,), (0,)), ((), ())),
        precision=lax.Precision.HIGHEST,
        preferred_element_type=jnp.float32,
    )


def times_transpose(left, right):
    return lax.dot_general(
        left, right, (((1,), (1,)), ((), ())), preferred_element_type=jnp.float32
    )


def gather_rows(block, axes):
    count = lax.axis_size(axes)
    copies = jnp.broadcast_to(block[None], (count,) + block.shape)
    gathered = lax.all_to_all(copies, axes, 0, 0, tiled=True)
    return gathered.reshape((count * block.shape[0],) + block.shape[1:])


def scatter_sum_rows(block, axes):
    count = lax.axis_size(axes)
    pieces = block.reshape((count, block.shape[0] // count) + block.shape[1:])
    return jnp.sum(lax.all_to_all(pieces, axes, 0, 0, tiled=True), axis=0)


def sum_everywhere(block):
    block = scatter_sum_rows(block, ("tile", "query"))
    count = lax.axis_size("dp")
    copies = jnp.broadcast_to(block[None], (count,) + block.shape)
    block = jnp.sum(lax.all_to_all(copies, "dp", 0, 0, tiled=True), axis=0)
    return gather_rows(block, ("tile", "query"))

def row_major(block):
    return with_layout_constraint(block, Layout(major_to_minor=(0, 1)))


def shift_down(block, offset):
    return jnp.concatenate(
        [jnp.zeros((offset, block.shape[1]), block.dtype), block[: block.shape[0] - offset]], axis=0
    )


def local(
    features,
    queries,
    out_grad,
    value_weight,
    attn_weight,
    out_weight,
    slot_point,
    slot_rows,
    slot_bilinear,
    slot_count,
):
    owners = lax.axis_size(("tile", "query"))
    page_count = lax.axis_size("dp")
    local_queries = queries.shape[1]
    all_queries = local_queries * owners
    grad_scale = float(page_count * all_queries) ** (-0.5)
    width = features.shape[2]
    att_width = attn_weight.shape[1]
    per_head = att_width // HEADS
    head_width = width // HEADS
    exponent = jnp.exp(
        jnp.dot(queries[0], attn_weight, preferred_element_type=jnp.float32)
    ).reshape(local_queries, HEADS, per_head)
    attention = (exponent / jnp.sum(exponent, axis=2, keepdims=True)).reshape(
        local_queries, att_width
    )
    attn_rounded = attention.astype(jnp.bfloat16)
    sample_grad = times_transpose(out_grad[0], out_weight).astype(jnp.bfloat16)
    every_both = gather_rows(
        jnp.concatenate([sample_grad, attn_rounded, out_grad[0]], axis=1), ("tile", "query")
    )
    every_grad = every_both[:, :width]
    every_attn = every_both[:, width : width + att_width]
    every_out = every_both[:, width + att_width :]
    projected = jnp.dot(features[0], value_weight, preferred_element_type=jnp.float32).astype(
        jnp.bfloat16
    )
    token_count = projected.shape[0]
    capacity = slot_point.shape[1]
    points = slot_point[0]
    alive_slot = jnp.arange(capacity, dtype=jnp.int32) < slot_count[0, 0]
    query_index = points // att_width
    attn_column = points % att_width
    head_index = attn_column // per_head
    query_match = query_index[:, None] == jnp.arange(all_queries, dtype=jnp.int32)[None, :]
    query_onehot = query_match.astype(jnp.bfloat16)
    column_match = attn_column[:, None] == jnp.arange(att_width, dtype=jnp.int32)[None, :]
    attn_rows = jnp.dot(query_onehot, every_attn, preferred_element_type=jnp.float32)
    picked_attn = jnp.sum(jnp.where(column_match, attn_rows, jnp.zeros((), jnp.float32)), axis=1)
    weight = jnp.where(alive_slot, picked_attn, jnp.zeros((), jnp.float32))
    head_mask = jnp.arange(width, dtype=jnp.int32)[None, :] // head_width == head_index[:, None]
    grad_rows = jnp.dot(query_onehot, every_grad, preferred_element_type=jnp.float32)
    slot_grad = row_major(jnp.where(head_mask, grad_rows, jnp.zeros((), jnp.float32)))
    offsets = (0, 1, TILE_W, TILE_W + 1)
    padded = jnp.concatenate([projected, jnp.zeros((TILE_W + 1, width), jnp.bfloat16)], axis=0)
    corner_table = jnp.concatenate(
        [padded[offset : offset + token_count] for offset in offsets], axis=1
    )
    base_row = slot_rows[0, 0]
    picked_all = row_major(corner_table[base_row]).astype(jnp.float32)
    mixed_rows = jnp.zeros((capacity, width), jnp.float32)
    contributions = []
    for corner in range(4):
        bilinear = slot_bilinear[0, corner]
        picked = picked_all[:, corner * width : (corner + 1) * width]
        mixed_rows = mixed_rows + bilinear[:, None] * picked
        contributions.append((weight * bilinear)[:, None] * slot_grad)
    corner_dots = jnp.sum(mixed_rows * slot_grad, axis=1)
    margin = TILE_W + 1
    corner_sums = (
        jnp.zeros((token_count + margin, 4 * width), jnp.float32)
        .at[base_row + margin]
        .add(row_major(jnp.concatenate(contributions, axis=1)))
    )
    value_grad = corner_sums[margin : margin + token_count, 0:width]
    for corner in range(1, 4):
        start = margin - offsets[corner]
        value_grad = (
            value_grad
            + corner_sums[start : start + token_count, corner * width : (corner + 1) * width]
        )
    query_float = query_match.astype(jnp.float32)
    sampled_part = over_rows_exact(
        query_float, jnp.where(head_mask, weight[:, None] * mixed_rows, jnp.zeros((), jnp.float32))
    )
    dots_table = jnp.where(
        jnp.logical_and(column_match, alive_slot[:, None]),
        corner_dots[:, None],
        jnp.zeros((), jnp.float32),
    )
    attn_part = over_rows_exact(query_float, dots_table)
    attn_grad = scatter_sum_rows(attn_part, ("tile", "query"))
    out_term = over_rows_exact(sampled_part, every_out.astype(jnp.float32))
    attn_three = attention.reshape(local_queries, HEADS, per_head)
    grad_three = attn_grad.reshape(local_queries, HEADS, per_head)
    logit_grad = (
        (attn_three * (grad_three - jnp.sum(attn_three * grad_three, axis=2, keepdims=True)))
        .reshape(local_queries, att_width)
        .astype(jnp.bfloat16)
    )
    query_grad = times_transpose(logit_grad, attn_weight).astype(jnp.bfloat16)
    value_rounded = value_grad.astype(jnp.bfloat16)
    feature_grad = times_transpose(value_rounded, value_weight).astype(jnp.bfloat16)
    value_term = over_rows(features[0], value_rounded)
    attn_term = over_rows(queries[0], logit_grad)
    summed = sum_everywhere(jnp.concatenate([value_term, attn_term, out_term], axis=1))
    return (
        feature_grad[None],
        query_grad[None],
        summed[:, :width] * grad_scale,
        summed[:, width : width + att_width] * grad_scale,
        summed[:, width + att_width :] * grad_scale,
    )


def solution(mesh):
    in_specs = (
        P("dp", ("tile", "query"), None),
        P("dp", ("tile", "query"), None),
        P("dp", ("tile", "query"), None),
        P(),
        P(),
        P(),
        P("dp", ("tile", "query")),
        P("dp", None, ("tile", "query")),
        P("dp", None, ("tile", "query")),
        P("dp", ("tile", "query")),
    )
    out_specs = (P("dp", ("tile", "query"), None), P("dp", ("tile", "query"), None), P(), P(), P())
    return jax.shard_map(local, mesh=mesh, in_specs=in_specs, out_specs=out_specs, check_vma=False)
```

```python
import jax
import jax.numpy as jnp
from jax import lax
from jax.experimental.layout import Layout, with_layout_constraint
from jax.sharding import PartitionSpec as P

HEADS = 8
TILE_W = 64


def over_rows(left, right):
    return lax.dot_general(
        left, right, (((0,), (0,)), ((), ())), preferred_element_type=jnp.float32
    )


def over_rows_exact(left, right):
    return lax.dot_general(
        left,
        right,
        (((0,), (0,)), ((), ())),
        precision=lax.Precision.HIGHEST,
        preferred_element_type=jnp.float32,
    )


def times_transpose(left, right):
    return lax.dot_general(
        left, right, (((1,), (1,)), ((), ())), preferred_element_type=jnp.float32
    )


def gather_rows(block, axes):
    count = lax.axis_size(axes)
    copies = jnp.broadcast_to(block[None], (count,) + block.shape)
    gathered = lax.all_to_all(copies, axes, 0, 0, tiled=True)
    return gathered.reshape((count * block.shape[0],) + block.shape[1:])


def scatter_sum_rows(block, axes):
    count = lax.axis_size(axes)
    pieces = block.reshape((count, block.shape[0] // count) + block.shape[1:])
    return jnp.sum(lax.all_to_all(pieces, axes, 0, 0, tiled=True), axis=0)


def sum_everywhere(block):
    block = scatter_sum_rows(block, ("tile", "query"))
    count = lax.axis_size("dp")
    copies = jnp.broadcast_to(block[None], (count,) + block.shape)
    block = jnp.sum(lax.all_to_all(copies, "dp", 0, 0, tiled=True), axis=0)
    return gather_rows(block, ("tile", "query"))

def row_major(block):
    return with_layout_constraint(block, Layout(major_to_minor=tuple(range(block.ndim))))


def shift_down(block, offset):
    return jnp.concatenate(
        [jnp.zeros((offset, block.shape[1]), block.dtype), block[: block.shape[0] - offset]], axis=0
    )


def local(
    features,
    queries,
    out_grad,
    value_weight,
    attn_weight,
    out_weight,
    slot_point,
    slot_rows,
    slot_bilinear,
    slot_count,
):
    owners = lax.axis_size(("tile", "query"))
    page_count = lax.axis_size("dp")
    local_queries = queries.shape[1]
    all_queries = local_queries * owners
    grad_scale = float(page_count * all_queries) ** (-0.5)
    width = features.shape[2]
    att_width = attn_weight.shape[1]
    per_head = att_width // HEADS
    head_width = width // HEADS
    exponent = jnp.exp(
        jnp.dot(queries[0], attn_weight, preferred_element_type=jnp.float32)
    ).reshape(local_queries, HEADS, per_head)
    attention = (exponent / jnp.sum(exponent, axis=2, keepdims=True)).reshape(
        local_queries, att_width
    )
    attn_rounded = attention.astype(jnp.bfloat16)
    sample_grad = times_transpose(out_grad[0], out_weight).astype(jnp.bfloat16)
    every_both = gather_rows(
        jnp.concatenate([sample_grad, attn_rounded, out_grad[0]], axis=1), ("tile", "query")
    )
    every_grad = every_both[:, :width]
    every_attn = every_both[:, width : width + att_width]
    every_out = every_both[:, width + att_width :]
    projected = jnp.dot(features[0], value_weight, preferred_element_type=jnp.float32).astype(
        jnp.bfloat16
    )
    token_count = projected.shape[0]
    capacity = slot_point.shape[1]
    points = slot_point[0]
    alive_slot = jnp.arange(capacity, dtype=jnp.int32) < slot_count[0, 0]
    query_index = points // att_width
    attn_column = points % att_width
    head_index = attn_column // per_head
    query_match = query_index[:, None] == jnp.arange(all_queries, dtype=jnp.int32)[None, :]
    query_onehot = query_match.astype(jnp.bfloat16)
    column_match = attn_column[:, None] == jnp.arange(att_width, dtype=jnp.int32)[None, :]
    attn_rows = jnp.dot(query_onehot, every_attn, preferred_element_type=jnp.float32)
    picked_attn = jnp.sum(jnp.where(column_match, attn_rows, jnp.zeros((), jnp.float32)), axis=1)
    weight = jnp.where(alive_slot, picked_attn, jnp.zeros((), jnp.float32))
    head_mask = jnp.arange(width, dtype=jnp.int32)[None, :] // head_width == head_index[:, None]
    grad_rows = jnp.dot(query_onehot, every_grad, preferred_element_type=jnp.float32)
    head_grad = jnp.zeros((capacity, head_width), jnp.float32)
    for head in range(HEADS):
        head_grad = jnp.where(
            (head_index == head)[:, None],
            grad_rows[:, head * head_width : (head + 1) * head_width],
            head_grad,
        )
    lanes = 4 * head_width
    grad_lanes = row_major(jnp.tile(head_grad, (1, 4)))
    offsets = (0, 1, TILE_W, TILE_W + 1)
    padded = jnp.concatenate([projected, jnp.zeros((TILE_W + 1, width), jnp.bfloat16)], axis=0)
    corner_table = row_major(
        jnp.stack([padded[offset : offset + token_count] for offset in offsets], axis=1)
        .reshape(token_count, 4, HEADS, head_width)
        .transpose(0, 2, 1, 3)
        .reshape(token_count, HEADS, lanes)
    ).reshape(token_count * HEADS, lanes)
    base_row = slot_rows[0, 0]
    picked = row_major(corner_table[base_row * HEADS + head_index]).astype(jnp.float32)
    bilinear_lanes = row_major(jnp.repeat(slot_bilinear[0].T, head_width, axis=1))
    weighted = picked * bilinear_lanes
    mixed_head = weighted[:, 0:head_width]
    for corner in range(1, 4):
        mixed_head = mixed_head + weighted[:, corner * head_width : (corner + 1) * head_width]
    corner_dots = jnp.sum(mixed_head * head_grad, axis=1)
    contributions = row_major((weight[:, None] * bilinear_lanes) * grad_lanes)
    margin = TILE_W + 1
    corner_sums = row_major(
        jnp.zeros(((token_count + margin) * HEADS, lanes), jnp.float32)
        .at[(base_row + margin) * HEADS + head_index]
        .add(contributions)
        .reshape(token_count + margin, HEADS, lanes)
    )
    value_grad = None
    for corner in range(4):
        start = margin - offsets[corner]
        block = corner_sums[
            start : start + token_count, :, corner * head_width : (corner + 1) * head_width
        ].reshape(token_count, width)
        value_grad = block if value_grad is None else value_grad + block
    value_grad = row_major(value_grad)
    mixed_rows = jnp.tile(mixed_head, (1, HEADS))
    query_float = query_match.astype(jnp.float32)
    sampled_part = over_rows_exact(
        query_float, jnp.where(head_mask, weight[:, None] * mixed_rows, jnp.zeros((), jnp.float32))
    )
    dots_table = jnp.where(
        jnp.logical_and(column_match, alive_slot[:, None]),
        corner_dots[:, None],
        jnp.zeros((), jnp.float32),
    )
    attn_part = over_rows_exact(query_float, dots_table)
    attn_grad = scatter_sum_rows(attn_part, ("tile", "query"))
    out_term = over_rows_exact(sampled_part, every_out.astype(jnp.float32))
    attn_three = attention.reshape(local_queries, HEADS, per_head)
    grad_three = attn_grad.reshape(local_queries, HEADS, per_head)
    logit_grad = (
        (attn_three * (grad_three - jnp.sum(attn_three * grad_three, axis=2, keepdims=True)))
        .reshape(local_queries, att_width)
        .astype(jnp.bfloat16)
    )
    query_grad = times_transpose(logit_grad, attn_weight).astype(jnp.bfloat16)
    value_rounded = value_grad.astype(jnp.bfloat16)
    feature_grad = times_transpose(value_rounded, value_weight).astype(jnp.bfloat16)
    value_term = over_rows(features[0], value_rounded)
    attn_term = over_rows(queries[0], logit_grad)
    summed = sum_everywhere(jnp.concatenate([value_term, attn_term, out_term], axis=1))
    return (
        feature_grad[None],
        query_grad[None],
        summed[:, :width] * grad_scale,
        summed[:, width : width + att_width] * grad_scale,
        summed[:, width + att_width :] * grad_scale,
    )


def solution(mesh):
    in_specs = (
        P("dp", ("tile", "query"), None),
        P("dp", ("tile", "query"), None),
        P("dp", ("tile", "query"), None),
        P(),
        P(),
        P(),
        P("dp", ("tile", "query")),
        P("dp", None, ("tile", "query")),
        P("dp", None, ("tile", "query")),
        P("dp", ("tile", "query")),
    )
    out_specs = (P("dp", ("tile", "query"), None), P("dp", ("tile", "query"), None), P(), P(), P())
    return jax.shard_map(local, mesh=mesh, in_specs=in_specs, out_specs=out_specs, check_vma=False)
```

```python
import jax
import jax.numpy as jnp
from jax import lax
from jax.experimental.layout import Layout, with_layout_constraint
from jax.sharding import PartitionSpec as P

HEADS = 8
TILE_W = 64


def over_rows(left, right):
    return lax.dot_general(
        left, right, (((0,), (0,)), ((), ())), preferred_element_type=jnp.float32
    )


def over_rows_exact(left, right):
    return lax.dot_general(
        left,
        right,
        (((0,), (0,)), ((), ())),
        precision=lax.Precision.HIGHEST,
        preferred_element_type=jnp.float32,
    )


def times_transpose(left, right):
    return lax.dot_general(
        left, right, (((1,), (1,)), ((), ())), preferred_element_type=jnp.float32
    )


def gather_rows(block, axes):
    count = lax.axis_size(axes)
    copies = jnp.broadcast_to(block[None], (count,) + block.shape)
    gathered = lax.all_to_all(copies, axes, 0, 0, tiled=True)
    return gathered.reshape((count * block.shape[0],) + block.shape[1:])


def scatter_sum_rows(block, axes):
    count = lax.axis_size(axes)
    pieces = block.reshape((count, block.shape[0] // count) + block.shape[1:])
    return jnp.sum(lax.all_to_all(pieces, axes, 0, 0, tiled=True), axis=0)


def sum_everywhere(block):
    count = lax.axis_size("dp")
    copies = jnp.broadcast_to(block[None], (count,) + block.shape)
    block = jnp.sum(lax.all_to_all(copies, "dp", 0, 0, tiled=True), axis=0)
    return gather_rows(block, ("tile", "query"))

def row_major(block):
    return with_layout_constraint(block, Layout(major_to_minor=(0, 1)))


def shift_down(block, offset):
    return jnp.concatenate(
        [jnp.zeros((offset, block.shape[1]), block.dtype), block[: block.shape[0] - offset]], axis=0
    )


def local(
    features,
    queries,
    out_grad,
    value_weight,
    attn_weight,
    out_weight,
    slot_point,
    slot_rows,
    slot_bilinear,
    slot_count,
):
    owners = lax.axis_size(("tile", "query"))
    page_count = lax.axis_size("dp")
    local_queries = queries.shape[1]
    all_queries = local_queries * owners
    grad_scale = float(page_count * all_queries) ** (-0.5)
    width = features.shape[2]
    att_width = attn_weight.shape[1]
    per_head = att_width // HEADS
    head_width = width // HEADS
    exponent = jnp.exp(
        jnp.dot(queries[0], attn_weight, preferred_element_type=jnp.float32)
    ).reshape(local_queries, HEADS, per_head)
    attention = (exponent / jnp.sum(exponent, axis=2, keepdims=True)).reshape(
        local_queries, att_width
    )
    attn_rounded = attention.astype(jnp.bfloat16)
    sample_grad = times_transpose(out_grad[0], out_weight).astype(jnp.bfloat16)
    every_both = gather_rows(
        jnp.concatenate([sample_grad, attn_rounded, out_grad[0], queries[0]], axis=1),
        ("tile", "query"),
    )
    every_grad = every_both[:, :width]
    every_attn = every_both[:, width : width + att_width]
    every_out = every_both[:, width + att_width : 2 * width + att_width]
    every_queries = every_both[:, 2 * width + att_width :]
    projected = jnp.dot(features[0], value_weight, preferred_element_type=jnp.float32).astype(
        jnp.bfloat16
    )
    token_count = projected.shape[0]
    capacity = slot_point.shape[1]
    points = slot_point[0]
    alive_slot = jnp.arange(capacity, dtype=jnp.int32) < slot_count[0, 0]
    query_index = points // att_width
    attn_column = points % att_width
    head_index = attn_column // per_head
    query_match = query_index[:, None] == jnp.arange(all_queries, dtype=jnp.int32)[None, :]
    query_onehot = query_match.astype(jnp.bfloat16)
    column_match = attn_column[:, None] == jnp.arange(att_width, dtype=jnp.int32)[None, :]
    attn_rows = jnp.dot(query_onehot, every_attn, preferred_element_type=jnp.float32)
    picked_attn = jnp.sum(jnp.where(column_match, attn_rows, jnp.zeros((), jnp.float32)), axis=1)
    weight = jnp.where(alive_slot, picked_attn, jnp.zeros((), jnp.float32))
    head_mask = jnp.arange(width, dtype=jnp.int32)[None, :] // head_width == head_index[:, None]
    grad_rows = jnp.dot(query_onehot, every_grad, preferred_element_type=jnp.float32)
    slot_grad = row_major(jnp.where(head_mask, grad_rows, jnp.zeros((), jnp.float32)))
    offsets = (0, 1, TILE_W, TILE_W + 1)
    padded = jnp.concatenate([projected, jnp.zeros((TILE_W + 1, width), jnp.bfloat16)], axis=0)
    corner_table = jnp.concatenate(
        [padded[offset : offset + token_count] for offset in offsets], axis=1
    )
    base_row = slot_rows[0, 0]
    picked_all = row_major(corner_table[base_row]).astype(jnp.float32)
    mixed_rows = jnp.zeros((capacity, width), jnp.float32)
    contributions = []
    for corner in range(4):
        bilinear = slot_bilinear[0, corner]
        picked = picked_all[:, corner * width : (corner + 1) * width]
        mixed_rows = mixed_rows + bilinear[:, None] * picked
        contributions.append((weight * bilinear)[:, None] * slot_grad)
    corner_dots = jnp.sum(mixed_rows * slot_grad, axis=1)
    margin = TILE_W + 1
    corner_sums = (
        jnp.zeros((token_count + margin, 4 * width), jnp.float32)
        .at[base_row + margin]
        .add(row_major(jnp.concatenate(contributions, axis=1)))
    )
    value_grad = corner_sums[margin : margin + token_count, 0:width]
    for corner in range(1, 4):
        start = margin - offsets[corner]
        value_grad = (
            value_grad
            + corner_sums[start : start + token_count, corner * width : (corner + 1) * width]
        )
    value_rounded = value_grad.astype(jnp.bfloat16)
    value_term = over_rows(features[0], value_rounded)
    query_float = query_match.astype(jnp.float32)
    sampled_part = over_rows_exact(
        query_float, jnp.where(head_mask, weight[:, None] * mixed_rows, jnp.zeros((), jnp.float32))
    )
    dots_table = jnp.where(
        jnp.logical_and(column_match, alive_slot[:, None]),
        corner_dots[:, None],
        jnp.zeros((), jnp.float32),
    )
    attn_part = over_rows_exact(query_float, dots_table)
    out_term = over_rows_exact(sampled_part, every_out.astype(jnp.float32))
    page_exponent = jnp.exp(
        jnp.dot(every_queries, attn_weight, preferred_element_type=jnp.float32)
    ).reshape(all_queries, HEADS, per_head)
    page_attention = page_exponent / jnp.sum(page_exponent, axis=2, keepdims=True)
    part_three = attn_part.reshape(all_queries, HEADS, per_head)
    part_logits = (
        page_attention
        * (part_three - jnp.sum(page_attention * part_three, axis=2, keepdims=True))
    ).reshape(all_queries, att_width)
    attn_term = over_rows_exact(every_queries.astype(jnp.float32), part_logits)
    terms = jnp.concatenate([value_term, attn_term, out_term], axis=1)
    shares = scatter_sum_rows(jnp.concatenate([terms, attn_part], axis=1), ("tile", "query"))
    attn_grad = shares[:, terms.shape[1] :]
    attn_three = attention.reshape(local_queries, HEADS, per_head)
    grad_three = attn_grad.reshape(local_queries, HEADS, per_head)
    logit_grad = (
        (attn_three * (grad_three - jnp.sum(attn_three * grad_three, axis=2, keepdims=True)))
        .reshape(local_queries, att_width)
        .astype(jnp.bfloat16)
    )
    query_grad = times_transpose(logit_grad, attn_weight).astype(jnp.bfloat16)
    feature_grad = times_transpose(value_rounded, value_weight).astype(jnp.bfloat16)
    summed = sum_everywhere(shares[:, : terms.shape[1]])
    return (
        feature_grad[None],
        query_grad[None],
        summed[:, :width] * grad_scale,
        summed[:, width : width + att_width] * grad_scale,
        summed[:, width + att_width :] * grad_scale,
    )


def solution(mesh):
    in_specs = (
        P("dp", ("tile", "query"), None),
        P("dp", ("tile", "query"), None),
        P("dp", ("tile", "query"), None),
        P(),
        P(),
        P(),
        P("dp", ("tile", "query")),
        P("dp", None, ("tile", "query")),
        P("dp", None, ("tile", "query")),
        P("dp", ("tile", "query")),
    )
    out_specs = (P("dp", ("tile", "query"), None), P("dp", ("tile", "query"), None), P(), P(), P())
    return jax.shard_map(local, mesh=mesh, in_specs=in_specs, out_specs=out_specs, check_vma=False)
```

```python
import jax
import jax.numpy as jnp
from jax import lax
from jax.experimental.layout import Layout, with_layout_constraint
from jax.sharding import PartitionSpec as P

HEADS = 8
TILE_W = 64


def over_rows(left, right):
    return lax.dot_general(
        left, right, (((0,), (0,)), ((), ())), preferred_element_type=jnp.float32
    )


def over_rows_exact(left, right):
    return lax.dot_general(
        left,
        right,
        (((0,), (0,)), ((), ())),
        precision=lax.Precision.HIGHEST,
        preferred_element_type=jnp.float32,
    )


def times_transpose(left, right):
    return lax.dot_general(
        left, right, (((1,), (1,)), ((), ())), preferred_element_type=jnp.float32
    )


def gather_rows(block, axes):
    count = lax.axis_size(axes)
    copies = jnp.broadcast_to(block[None], (count,) + block.shape)
    gathered = lax.all_to_all(copies, axes, 0, 0, tiled=True)
    return gathered.reshape((count * block.shape[0],) + block.shape[1:])


def scatter_sum_rows(block, axes):
    count = lax.axis_size(axes)
    pieces = block.reshape((count, block.shape[0] // count) + block.shape[1:])
    return jnp.sum(lax.all_to_all(pieces, axes, 0, 0, tiled=True), axis=0)


def sum_everywhere(block):
    count = lax.axis_size("dp")
    copies = jnp.broadcast_to(block[None], (count,) + block.shape)
    block = jnp.sum(lax.all_to_all(copies, "dp", 0, 0, tiled=True), axis=0)
    return gather_rows(block, ("tile", "query"))

def row_major(block):
    return with_layout_constraint(block, Layout(major_to_minor=(0, 1)))


def shift_down(block, offset):
    return jnp.concatenate(
        [jnp.zeros((offset, block.shape[1]), block.dtype), block[: block.shape[0] - offset]], axis=0
    )


def local(
    features,
    queries,
    out_grad,
    value_weight,
    attn_weight,
    out_weight,
    slot_point,
    slot_rows,
    slot_bilinear,
    slot_count,
):
    owners = lax.axis_size(("tile", "query"))
    page_count = lax.axis_size("dp")
    local_queries = queries.shape[1]
    all_queries = local_queries * owners
    grad_scale = float(page_count * all_queries) ** (-0.5)
    width = features.shape[2]
    att_width = attn_weight.shape[1]
    per_head = att_width // HEADS
    head_width = width // HEADS
    exponent = jnp.exp(
        jnp.dot(queries[0], attn_weight, preferred_element_type=jnp.float32)
    ).reshape(local_queries, HEADS, per_head)
    attention = (exponent / jnp.sum(exponent, axis=2, keepdims=True)).reshape(
        local_queries, att_width
    )
    attn_rounded = attention.astype(jnp.bfloat16)
    sample_grad = times_transpose(out_grad[0], out_weight).astype(jnp.bfloat16)
    every_both = gather_rows(
        jnp.concatenate([sample_grad, attn_rounded, out_grad[0], queries[0]], axis=1),
        ("tile", "query"),
    )
    every_grad = every_both[:, :width]
    every_attn = every_both[:, width : width + att_width]
    every_out = every_both[:, width + att_width : 2 * width + att_width]
    every_queries = every_both[:, 2 * width + att_width :]
    projected = jnp.dot(features[0], value_weight, preferred_element_type=jnp.float32).astype(
        jnp.bfloat16
    )
    token_count = projected.shape[0]
    capacity = slot_point.shape[1]
    points = slot_point[0]
    alive_slot = jnp.arange(capacity, dtype=jnp.int32) < slot_count[0, 0]
    query_index = points // att_width
    attn_column = points % att_width
    head_index = attn_column // per_head
    query_match = query_index[:, None] == jnp.arange(all_queries, dtype=jnp.int32)[None, :]
    query_onehot = query_match.astype(jnp.bfloat16)
    column_match = attn_column[:, None] == jnp.arange(att_width, dtype=jnp.int32)[None, :]
    attn_rows = jnp.dot(query_onehot, every_attn, preferred_element_type=jnp.float32)
    picked_attn = jnp.sum(jnp.where(column_match, attn_rows, jnp.zeros((), jnp.float32)), axis=1)
    weight = jnp.where(alive_slot, picked_attn, jnp.zeros((), jnp.float32))
    head_mask = jnp.arange(width, dtype=jnp.int32)[None, :] // head_width == head_index[:, None]
    grad_rows = jnp.dot(query_onehot, every_grad, preferred_element_type=jnp.float32)
    slot_grad = row_major(jnp.where(head_mask, grad_rows, jnp.zeros((), jnp.float32)))
    offsets = (0, 1, TILE_W, TILE_W + 1)
    padded = jnp.concatenate(
        [
            jnp.concatenate([projected, features[0]], axis=1),
            jnp.zeros((TILE_W + 1, 2 * width), jnp.bfloat16),
        ],
        axis=0,
    )
    corner_table = jnp.concatenate(
        [padded[offset : offset + token_count] for offset in offsets], axis=1
    )
    base_row = slot_rows[0, 0]
    picked_all = row_major(corner_table[base_row]).astype(jnp.float32)
    mixed_rows = jnp.zeros((capacity, width), jnp.float32)
    mixed_features = jnp.zeros((capacity, width), jnp.float32)
    contributions = []
    for corner in range(4):
        bilinear = slot_bilinear[0, corner]
        picked = picked_all[:, 2 * corner * width : (2 * corner + 1) * width]
        picked_features = picked_all[:, (2 * corner + 1) * width : (2 * corner + 2) * width]
        mixed_rows = mixed_rows + bilinear[:, None] * picked
        mixed_features = mixed_features + bilinear[:, None] * picked_features
        contributions.append((weight * bilinear)[:, None] * slot_grad)
    value_term = over_rows_exact(mixed_features, weight[:, None] * slot_grad)
    corner_dots = jnp.sum(mixed_rows * slot_grad, axis=1)
    margin = TILE_W + 1
    corner_sums = (
        jnp.zeros((token_count + margin, 4 * width), jnp.float32)
        .at[base_row + margin]
        .add(row_major(jnp.concatenate(contributions, axis=1)))
    )
    value_grad = corner_sums[margin : margin + token_count, 0:width]
    for corner in range(1, 4):
        start = margin - offsets[corner]
        value_grad = (
            value_grad
            + corner_sums[start : start + token_count, corner * width : (corner + 1) * width]
        )
    value_rounded = value_grad.astype(jnp.bfloat16)
    query_float = query_match.astype(jnp.float32)
    sampled_part = over_rows_exact(
        query_float, jnp.where(head_mask, weight[:, None] * mixed_rows, jnp.zeros((), jnp.float32))
    )
    dots_table = jnp.where(
        jnp.logical_and(column_match, alive_slot[:, None]),
        corner_dots[:, None],
        jnp.zeros((), jnp.float32),
    )
    attn_part = over_rows_exact(query_float, dots_table)
    out_term = over_rows_exact(sampled_part, every_out.astype(jnp.float32))
    page_exponent = jnp.exp(
        jnp.dot(every_queries, attn_weight, preferred_element_type=jnp.float32)
    ).reshape(all_queries, HEADS, per_head)
    page_attention = page_exponent / jnp.sum(page_exponent, axis=2, keepdims=True)
    part_three = attn_part.reshape(all_queries, HEADS, per_head)
    part_logits = (
        page_attention
        * (part_three - jnp.sum(page_attention * part_three, axis=2, keepdims=True))
    ).reshape(all_queries, att_width)
    attn_term = over_rows_exact(every_queries.astype(jnp.float32), part_logits)
    terms = jnp.concatenate([value_term, attn_term, out_term], axis=1)
    shares = scatter_sum_rows(jnp.concatenate([terms, attn_part], axis=1), ("tile", "query"))
    attn_grad = shares[:, terms.shape[1] :]
    attn_three = attention.reshape(local_queries, HEADS, per_head)
    grad_three = attn_grad.reshape(local_queries, HEADS, per_head)
    logit_grad = (
        (attn_three * (grad_three - jnp.sum(attn_three * grad_three, axis=2, keepdims=True)))
        .reshape(local_queries, att_width)
        .astype(jnp.bfloat16)
    )
    query_grad = times_transpose(logit_grad, attn_weight).astype(jnp.bfloat16)
    feature_grad = times_transpose(value_rounded, value_weight).astype(jnp.bfloat16)
    summed = sum_everywhere(shares[:, : terms.shape[1]])
    return (
        feature_grad[None],
        query_grad[None],
        summed[:, :width] * grad_scale,
        summed[:, width : width + att_width] * grad_scale,
        summed[:, width + att_width :] * grad_scale,
    )


def solution(mesh):
    in_specs = (
        P("dp", ("tile", "query"), None),
        P("dp", ("tile", "query"), None),
        P("dp", ("tile", "query"), None),
        P(),
        P(),
        P(),
        P("dp", ("tile", "query")),
        P("dp", None, ("tile", "query")),
        P("dp", None, ("tile", "query")),
        P("dp", ("tile", "query")),
    )
    out_specs = (P("dp", ("tile", "query"), None), P("dp", ("tile", "query"), None), P(), P(), P())
    return jax.shard_map(local, mesh=mesh, in_specs=in_specs, out_specs=out_specs, check_vma=False)
```

```python
import jax
import jax.numpy as jnp
from jax import lax
from jax.experimental.layout import Layout, with_layout_constraint
from jax.sharding import PartitionSpec as P

HEADS = 8
TILE_W = 64


def over_rows(left, right):
    return lax.dot_general(
        left, right, (((0,), (0,)), ((), ())), preferred_element_type=jnp.float32
    )


def over_rows_exact(left, right):
    return lax.dot_general(
        left,
        right,
        (((0,), (0,)), ((), ())),
        precision=lax.Precision.HIGHEST,
        preferred_element_type=jnp.float32,
    )


def times_transpose(left, right):
    return lax.dot_general(
        left, right, (((1,), (1,)), ((), ())), preferred_element_type=jnp.float32
    )


def gather_rows(block, axes):
    count = lax.axis_size(axes)
    copies = jnp.broadcast_to(block[None], (count,) + block.shape)
    gathered = lax.all_to_all(copies, axes, 0, 0, tiled=True)
    return gathered.reshape((count * block.shape[0],) + block.shape[1:])


def scatter_sum_rows(block, axes):
    count = lax.axis_size(axes)
    pieces = block.reshape((count, block.shape[0] // count) + block.shape[1:])
    return jnp.sum(lax.all_to_all(pieces, axes, 0, 0, tiled=True), axis=0)


def sum_everywhere(block):
    count = lax.axis_size("dp")
    copies = jnp.broadcast_to(block[None], (count,) + block.shape)
    block = jnp.sum(lax.all_to_all(copies, "dp", 0, 0, tiled=True), axis=0)
    return gather_rows(block, ("tile", "query"))

def row_major(block):
    return with_layout_constraint(block, Layout(major_to_minor=(0, 1)))


def shift_down(block, offset):
    return jnp.concatenate(
        [jnp.zeros((offset, block.shape[1]), block.dtype), block[: block.shape[0] - offset]], axis=0
    )


def local(
    features,
    queries,
    out_grad,
    value_weight,
    attn_weight,
    out_weight,
    slot_point,
    slot_rows,
    slot_bilinear,
    slot_count,
):
    owners = lax.axis_size(("tile", "query"))
    page_count = lax.axis_size("dp")
    local_queries = queries.shape[1]
    all_queries = local_queries * owners
    grad_scale = float(page_count * all_queries) ** (-0.5)
    width = features.shape[2]
    att_width = attn_weight.shape[1]
    per_head = att_width // HEADS
    head_width = width // HEADS
    exponent = jnp.exp(
        jnp.dot(queries[0], attn_weight, preferred_element_type=jnp.float32)
    ).reshape(local_queries, HEADS, per_head)
    attention = (exponent / jnp.sum(exponent, axis=2, keepdims=True)).reshape(
        local_queries, att_width
    )
    attn_rounded = attention.astype(jnp.bfloat16)
    sample_grad = times_transpose(out_grad[0], out_weight).astype(jnp.bfloat16)
    every_both = gather_rows(
        jnp.concatenate([sample_grad, attn_rounded, out_grad[0], queries[0]], axis=1),
        ("tile", "query"),
    )
    every_grad = every_both[:, :width]
    every_attn = every_both[:, width : width + att_width]
    every_out = every_both[:, width + att_width : 2 * width + att_width]
    every_queries = every_both[:, 2 * width + att_width :]
    projected = jnp.dot(features[0], value_weight, preferred_element_type=jnp.float32).astype(
        jnp.bfloat16
    )
    token_count = projected.shape[0]
    capacity = slot_point.shape[1]
    points = slot_point[0]
    alive_slot = jnp.arange(capacity, dtype=jnp.int32) < slot_count[0, 0]
    query_index = points // att_width
    attn_column = points % att_width
    head_index = attn_column // per_head
    query_match = query_index[:, None] == jnp.arange(all_queries, dtype=jnp.int32)[None, :]
    query_onehot = query_match.astype(jnp.bfloat16)
    column_match = attn_column[:, None] == jnp.arange(att_width, dtype=jnp.int32)[None, :]
    attn_rows = jnp.dot(query_onehot, every_attn, preferred_element_type=jnp.float32)
    picked_attn = jnp.sum(jnp.where(column_match, attn_rows, jnp.zeros((), jnp.float32)), axis=1)
    weight = jnp.where(alive_slot, picked_attn, jnp.zeros((), jnp.float32))
    head_mask = jnp.arange(width, dtype=jnp.int32)[None, :] // head_width == head_index[:, None]
    grad_rows = jnp.dot(query_onehot, every_grad, preferred_element_type=jnp.float32)
    slot_grad = row_major(jnp.where(head_mask, grad_rows, jnp.zeros((), jnp.float32)))
    offsets = (0, 1, TILE_W, TILE_W + 1)
    padded = jnp.concatenate([projected, jnp.zeros((TILE_W + 1, width), jnp.bfloat16)], axis=0)
    corner_table = jnp.concatenate(
        [padded[offset : offset + token_count] for offset in offsets], axis=1
    )
    base_row = slot_rows[0, 0]
    picked_all = row_major(corner_table[base_row]).astype(jnp.float32)
    mixed_rows = jnp.zeros((capacity, width), jnp.float32)
    contributions = []
    for corner in range(4):
        bilinear = slot_bilinear[0, corner]
        picked = picked_all[:, corner * width : (corner + 1) * width]
        mixed_rows = mixed_rows + bilinear[:, None] * picked
        contributions.append((weight * bilinear)[:, None] * slot_grad)
    corner_dots = jnp.sum(mixed_rows * slot_grad, axis=1)
    margin = TILE_W + 1
    corner_sums = (
        jnp.zeros((token_count + margin, 4 * width), jnp.float32)
        .at[base_row + margin]
        .add(row_major(jnp.concatenate(contributions, axis=1)))
    )
    value_grad = corner_sums[margin : margin + token_count, 0:width]
    for corner in range(1, 4):
        start = margin - offsets[corner]
        value_grad = (
            value_grad
            + corner_sums[start : start + token_count, corner * width : (corner + 1) * width]
        )
    value_rounded = value_grad.astype(jnp.bfloat16)
    value_term = over_rows(features[0], value_rounded)
    query_float = query_match.astype(jnp.float32)
    sampled_part = over_rows_exact(
        query_float, jnp.where(head_mask, weight[:, None] * mixed_rows, jnp.zeros((), jnp.float32))
    )
    dots_table = jnp.where(
        jnp.logical_and(column_match, alive_slot[:, None]),
        corner_dots[:, None],
        jnp.zeros((), jnp.float32),
    )
    attn_part = over_rows_exact(query_float, dots_table)
    out_term = over_rows_exact(sampled_part, every_out.astype(jnp.float32))
    page_exponent = jnp.exp(
        jnp.dot(every_queries, attn_weight, preferred_element_type=jnp.float32)
    ).reshape(all_queries, HEADS, per_head)
    page_attention = page_exponent / jnp.sum(page_exponent, axis=2, keepdims=True)
    part_three = attn_part.reshape(all_queries, HEADS, per_head)
    part_logits = (
        page_attention
        * (part_three - jnp.sum(page_attention * part_three, axis=2, keepdims=True))
    ).reshape(all_queries, att_width)
    attn_term = over_rows_exact(every_queries.astype(jnp.float32), part_logits)
    terms = jnp.concatenate([value_term, attn_term, out_term], axis=1) * grad_scale
    shares = scatter_sum_rows(jnp.concatenate([terms, attn_part], axis=1), ("tile", "query"))
    attn_grad = shares[:, terms.shape[1] :]
    attn_three = attention.reshape(local_queries, HEADS, per_head)
    grad_three = attn_grad.reshape(local_queries, HEADS, per_head)
    logit_grad = (
        (attn_three * (grad_three - jnp.sum(attn_three * grad_three, axis=2, keepdims=True)))
        .reshape(local_queries, att_width)
        .astype(jnp.bfloat16)
    )
    query_grad = times_transpose(logit_grad, attn_weight).astype(jnp.bfloat16)
    feature_grad = times_transpose(value_rounded, value_weight).astype(jnp.bfloat16)
    summed = sum_everywhere(shares[:, : terms.shape[1]])
    return (
        feature_grad[None],
        query_grad[None],
        summed[:, :width],
        summed[:, width : width + att_width],
        summed[:, width + att_width :],
    )


def solution(mesh):
    in_specs = (
        P("dp", ("tile", "query"), None),
        P("dp", ("tile", "query"), None),
        P("dp", ("tile", "query"), None),
        P(),
        P(),
        P(),
        P("dp", ("tile", "query")),
        P("dp", None, ("tile", "query")),
        P("dp", None, ("tile", "query")),
        P("dp", ("tile", "query")),
    )
    out_specs = (P("dp", ("tile", "query"), None), P("dp", ("tile", "query"), None), P(), P(), P())
    return jax.shard_map(local, mesh=mesh, in_specs=in_specs, out_specs=out_specs, check_vma=False)
```

```python
import jax
import jax.numpy as jnp
from jax import lax
from jax.experimental.layout import Layout, with_layout_constraint
from jax.sharding import PartitionSpec as P

HEADS = 8
TILE_W = 64


def over_rows(left, right):
    return lax.dot_general(
        left, right, (((0,), (0,)), ((), ())), preferred_element_type=jnp.float32
    )


def over_rows_exact(left, right):
    return lax.dot_general(
        left,
        right,
        (((0,), (0,)), ((), ())),
        precision=lax.Precision.HIGHEST,
        preferred_element_type=jnp.float32,
    )


def times_transpose(left, right):
    return lax.dot_general(
        left, right, (((1,), (1,)), ((), ())), preferred_element_type=jnp.float32
    )


def gather_rows(block, axes):
    count = lax.axis_size(axes)
    copies = jnp.broadcast_to(block[None], (count,) + block.shape)
    gathered = lax.all_to_all(copies, axes, 0, 0, tiled=True)
    return gathered.reshape((count * block.shape[0],) + block.shape[1:])


def scatter_sum_rows(block, axes):
    count = lax.axis_size(axes)
    pieces = block.reshape((count, block.shape[0] // count) + block.shape[1:])
    return jnp.sum(lax.all_to_all(pieces, axes, 0, 0, tiled=True), axis=0)


def sum_everywhere(block):
    count = lax.axis_size("dp")
    copies = jnp.broadcast_to(block[None], (count,) + block.shape)
    block = jnp.sum(lax.all_to_all(copies, "dp", 0, 0, tiled=True), axis=0)
    return gather_rows(block, ("tile", "query"))

def row_major(block):
    return with_layout_constraint(block, Layout(major_to_minor=(0, 1)))


def shift_down(block, offset):
    return jnp.concatenate(
        [jnp.zeros((offset, block.shape[1]), block.dtype), block[: block.shape[0] - offset]], axis=0
    )


def local(
    features,
    queries,
    out_grad,
    value_weight,
    attn_weight,
    out_weight,
    slot_point,
    slot_rows,
    slot_bilinear,
    slot_count,
):
    owners = lax.axis_size(("tile", "query"))
    page_count = lax.axis_size("dp")
    local_queries = queries.shape[1]
    all_queries = local_queries * owners
    grad_scale = float(page_count * all_queries) ** (-0.5)
    width = features.shape[2]
    att_width = attn_weight.shape[1]
    per_head = att_width // HEADS
    head_width = width // HEADS
    exponent = jnp.exp(
        jnp.dot(queries[0], attn_weight, preferred_element_type=jnp.float32)
    ).reshape(local_queries, HEADS, per_head)
    attention = (exponent / jnp.sum(exponent, axis=2, keepdims=True)).reshape(
        local_queries, att_width
    )
    attn_rounded = attention.astype(jnp.bfloat16)
    sample_grad = times_transpose(out_grad[0], out_weight).astype(jnp.bfloat16)
    every_both = gather_rows(
        jnp.concatenate([sample_grad, attn_rounded, out_grad[0], queries[0]], axis=1),
        ("tile", "query"),
    )
    every_grad = every_both[:, :width]
    every_attn = every_both[:, width : width + att_width]
    every_out = every_both[:, width + att_width : 2 * width + att_width]
    every_queries = every_both[:, 2 * width + att_width :]
    projected = jnp.dot(features[0], value_weight, preferred_element_type=jnp.float32).astype(
        jnp.bfloat16
    )
    token_count = projected.shape[0]
    capacity = slot_point.shape[1]
    points = slot_point[0]
    alive_slot = jnp.arange(capacity, dtype=jnp.int32) < slot_count[0, 0]
    query_index = points // att_width
    attn_column = points % att_width
    head_index = attn_column // per_head
    query_match = query_index[:, None] == jnp.arange(all_queries, dtype=jnp.int32)[None, :]
    query_onehot = query_match.astype(jnp.bfloat16)
    column_match = attn_column[:, None] == jnp.arange(att_width, dtype=jnp.int32)[None, :]
    attn_rows = jnp.dot(query_onehot, every_attn, preferred_element_type=jnp.float32)
    picked_attn = jnp.sum(jnp.where(column_match, attn_rows, jnp.zeros((), jnp.float32)), axis=1)
    weight = jnp.where(alive_slot, picked_attn, jnp.zeros((), jnp.float32))
    head_mask = jnp.arange(width, dtype=jnp.int32)[None, :] // head_width == head_index[:, None]
    grad_rows = jnp.dot(query_onehot, every_grad, preferred_element_type=jnp.float32)
    slot_grad = row_major(jnp.where(head_mask, grad_rows, jnp.zeros((), jnp.float32)))
    offsets = (0, 1, TILE_W, TILE_W + 1)
    padded = jnp.concatenate([projected, jnp.zeros((TILE_W + 1, width), jnp.bfloat16)], axis=0)
    corner_table = jnp.concatenate(
        [padded[offset : offset + token_count] for offset in offsets], axis=1
    )
    base_row = slot_rows[0, 0]
    picked_all = row_major(corner_table[base_row])
    mixed_rows = jnp.zeros((capacity, width), jnp.float32)
    contributions = []
    for corner in range(4):
        bilinear = slot_bilinear[0, corner]
        picked = picked_all[:, corner * width : (corner + 1) * width].astype(jnp.float32)
        mixed_rows = mixed_rows + bilinear[:, None] * picked
        contributions.append((weight * bilinear)[:, None] * slot_grad)
    corner_dots = jnp.sum(mixed_rows * slot_grad, axis=1)
    margin = TILE_W + 1
    corner_sums = (
        jnp.zeros((token_count + margin, 4 * width), jnp.float32)
        .at[base_row + margin]
        .add(row_major(jnp.concatenate(contributions, axis=1)))
    )
    value_grad = corner_sums[margin : margin + token_count, 0:width]
    for corner in range(1, 4):
        start = margin - offsets[corner]
        value_grad = (
            value_grad
            + corner_sums[start : start + token_count, corner * width : (corner + 1) * width]
        )
    value_rounded = value_grad.astype(jnp.bfloat16)
    value_term = over_rows(features[0], value_rounded)
    query_float = query_match.astype(jnp.float32)
    sampled_part = over_rows_exact(
        query_float, jnp.where(head_mask, weight[:, None] * mixed_rows, jnp.zeros((), jnp.float32))
    )
    dots_table = jnp.where(
        jnp.logical_and(column_match, alive_slot[:, None]),
        corner_dots[:, None],
        jnp.zeros((), jnp.float32),
    )
    attn_part = over_rows_exact(query_float, dots_table)
    out_term = over_rows_exact(sampled_part, every_out.astype(jnp.float32))
    page_exponent = jnp.exp(
        jnp.dot(every_queries, attn_weight, preferred_element_type=jnp.float32)
    ).reshape(all_queries, HEADS, per_head)
    page_attention = page_exponent / jnp.sum(page_exponent, axis=2, keepdims=True)
    part_three = attn_part.reshape(all_queries, HEADS, per_head)
    part_logits = (
        page_attention
        * (part_three - jnp.sum(page_attention * part_three, axis=2, keepdims=True))
    ).reshape(all_queries, att_width)
    attn_term = over_rows_exact(every_queries.astype(jnp.float32), part_logits)
    terms = jnp.concatenate([value_term, attn_term, out_term], axis=1) * grad_scale
    shares = scatter_sum_rows(jnp.concatenate([terms, attn_part], axis=1), ("tile", "query"))
    attn_grad = shares[:, terms.shape[1] :]
    attn_three = attention.reshape(local_queries, HEADS, per_head)
    grad_three = attn_grad.reshape(local_queries, HEADS, per_head)
    logit_grad = (
        (attn_three * (grad_three - jnp.sum(attn_three * grad_three, axis=2, keepdims=True)))
        .reshape(local_queries, att_width)
        .astype(jnp.bfloat16)
    )
    query_grad = times_transpose(logit_grad, attn_weight).astype(jnp.bfloat16)
    feature_grad = times_transpose(value_rounded, value_weight).astype(jnp.bfloat16)
    summed = sum_everywhere(shares[:, : terms.shape[1]])
    return (
        feature_grad[None],
        query_grad[None],
        summed[:, :width],
        summed[:, width : width + att_width],
        summed[:, width + att_width :],
    )


def solution(mesh):
    in_specs = (
        P("dp", ("tile", "query"), None),
        P("dp", ("tile", "query"), None),
        P("dp", ("tile", "query"), None),
        P(),
        P(),
        P(),
        P("dp", ("tile", "query")),
        P("dp", None, ("tile", "query")),
        P("dp", None, ("tile", "query")),
        P("dp", ("tile", "query")),
    )
    out_specs = (P("dp", ("tile", "query"), None), P("dp", ("tile", "query"), None), P(), P(), P())
    return jax.shard_map(local, mesh=mesh, in_specs=in_specs, out_specs=out_specs, check_vma=False)
```

```python
import jax
import jax.numpy as jnp
from jax import lax
from jax.experimental.layout import Layout, with_layout_constraint
from jax.sharding import PartitionSpec as P

HEADS = 8
TILE_W = 64


def over_rows(left, right):
    return lax.dot_general(
        left, right, (((0,), (0,)), ((), ())), preferred_element_type=jnp.float32
    )


def over_rows_exact(left, right):
    return lax.dot_general(
        left,
        right,
        (((0,), (0,)), ((), ())),
        precision=lax.Precision.HIGHEST,
        preferred_element_type=jnp.float32,
    )


def times_transpose(left, right):
    return lax.dot_general(
        left, right, (((1,), (1,)), ((), ())), preferred_element_type=jnp.float32
    )


def gather_rows(block, axes):
    count = lax.axis_size(axes)
    copies = jnp.broadcast_to(block[None], (count,) + block.shape)
    gathered = lax.all_to_all(copies, axes, 0, 0, tiled=True)
    return gathered.reshape((count * block.shape[0],) + block.shape[1:])


def scatter_sum_rows(block, axes):
    count = lax.axis_size(axes)
    pieces = block.reshape((count, block.shape[0] // count) + block.shape[1:])
    return jnp.sum(lax.all_to_all(pieces, axes, 0, 0, tiled=True), axis=0)


def sum_everywhere(block):
    count = lax.axis_size("dp")
    copies = jnp.broadcast_to(block[None], (count,) + block.shape)
    block = jnp.sum(lax.all_to_all(copies, "dp", 0, 0, tiled=True), axis=0)
    return gather_rows(block, ("tile", "query"))

def row_major(block):
    return with_layout_constraint(block, Layout(major_to_minor=(0, 1)))


def shift_down(block, offset):
    return jnp.concatenate(
        [jnp.zeros((offset, block.shape[1]), block.dtype), block[: block.shape[0] - offset]], axis=0
    )


def local(
    features,
    queries,
    out_grad,
    value_weight,
    attn_weight,
    out_weight,
    slot_point,
    slot_rows,
    slot_bilinear,
    slot_count,
):
    owners = lax.axis_size(("tile", "query"))
    page_count = lax.axis_size("dp")
    local_queries = queries.shape[1]
    all_queries = local_queries * owners
    grad_scale = float(page_count * all_queries) ** (-0.5)
    width = features.shape[2]
    att_width = attn_weight.shape[1]
    per_head = att_width // HEADS
    head_width = width // HEADS
    exponent = jnp.exp(
        jnp.dot(queries[0], attn_weight, preferred_element_type=jnp.float32)
    ).reshape(local_queries, HEADS, per_head)
    attention = (exponent / jnp.sum(exponent, axis=2, keepdims=True)).reshape(
        local_queries, att_width
    )
    sample_grad = times_transpose(out_grad[0], out_weight).astype(jnp.bfloat16)
    every_both = gather_rows(
        jnp.concatenate([sample_grad, out_grad[0], queries[0]], axis=1), ("tile", "query")
    )
    every_grad = every_both[:, :width]
    every_out = every_both[:, width : 2 * width]
    every_queries = every_both[:, 2 * width :]
    page_exponent = jnp.exp(
        jnp.dot(every_queries, attn_weight, preferred_element_type=jnp.float32)
    ).reshape(all_queries, HEADS, per_head)
    page_attention = page_exponent / jnp.sum(page_exponent, axis=2, keepdims=True)
    every_attn = page_attention.reshape(all_queries, att_width).astype(jnp.bfloat16)
    projected = jnp.dot(features[0], value_weight, preferred_element_type=jnp.float32).astype(
        jnp.bfloat16
    )
    token_count = projected.shape[0]
    capacity = slot_point.shape[1]
    points = slot_point[0]
    alive_slot = jnp.arange(capacity, dtype=jnp.int32) < slot_count[0, 0]
    query_index = points // att_width
    attn_column = points % att_width
    head_index = attn_column // per_head
    query_match = query_index[:, None] == jnp.arange(all_queries, dtype=jnp.int32)[None, :]
    query_onehot = query_match.astype(jnp.bfloat16)
    column_match = attn_column[:, None] == jnp.arange(att_width, dtype=jnp.int32)[None, :]
    attn_rows = jnp.dot(query_onehot, every_attn, preferred_element_type=jnp.float32)
    picked_attn = jnp.sum(jnp.where(column_match, attn_rows, jnp.zeros((), jnp.float32)), axis=1)
    weight = jnp.where(alive_slot, picked_attn, jnp.zeros((), jnp.float32))
    head_mask = jnp.arange(width, dtype=jnp.int32)[None, :] // head_width == head_index[:, None]
    grad_rows = jnp.dot(query_onehot, every_grad, preferred_element_type=jnp.float32)
    slot_grad = row_major(jnp.where(head_mask, grad_rows, jnp.zeros((), jnp.float32)))
    offsets = (0, 1, TILE_W, TILE_W + 1)
    padded = jnp.concatenate([projected, jnp.zeros((TILE_W + 1, width), jnp.bfloat16)], axis=0)
    corner_table = jnp.concatenate(
        [padded[offset : offset + token_count] for offset in offsets], axis=1
    )
    base_row = slot_rows[0, 0]
    picked_all = row_major(corner_table[base_row])
    mixed_rows = jnp.zeros((capacity, width), jnp.float32)
    contributions = []
    for corner in range(4):
        bilinear = slot_bilinear[0, corner]
        picked = picked_all[:, corner * width : (corner + 1) * width].astype(jnp.float32)
        mixed_rows = mixed_rows + bilinear[:, None] * picked
        contributions.append((weight * bilinear)[:, None] * slot_grad)
    corner_dots = jnp.sum(mixed_rows * slot_grad, axis=1)
    margin = TILE_W + 1
    corner_sums = (
        jnp.zeros((token_count + margin, 4 * width), jnp.float32)
        .at[base_row + margin]
        .add(row_major(jnp.concatenate(contributions, axis=1)))
    )
    value_grad = corner_sums[margin : margin + token_count, 0:width]
    for corner in range(1, 4):
        start = margin - offsets[corner]
        value_grad = (
            value_grad
            + corner_sums[start : start + token_count, corner * width : (corner + 1) * width]
        )
    value_rounded = value_grad.astype(jnp.bfloat16)
    value_term = over_rows(features[0], value_rounded)
    query_float = query_match.astype(jnp.float32)
    sampled_part = over_rows_exact(
        query_float, jnp.where(head_mask, weight[:, None] * mixed_rows, jnp.zeros((), jnp.float32))
    )
    dots_table = jnp.where(
        jnp.logical_and(column_match, alive_slot[:, None]),
        corner_dots[:, None],
        jnp.zeros((), jnp.float32),
    )
    attn_part = over_rows_exact(query_float, dots_table)
    out_term = over_rows_exact(sampled_part, every_out.astype(jnp.float32))
    part_three = attn_part.reshape(all_queries, HEADS, per_head)
    part_logits = (
        page_attention
        * (part_three - jnp.sum(page_attention * part_three, axis=2, keepdims=True))
    ).reshape(all_queries, att_width)
    attn_term = over_rows_exact(every_queries.astype(jnp.float32), part_logits)
    terms = jnp.concatenate([value_term, attn_term, out_term], axis=1) * grad_scale
    shares = scatter_sum_rows(jnp.concatenate([terms, attn_part], axis=1), ("tile", "query"))
    attn_grad = shares[:, terms.shape[1] :]
    attn_three = attention.reshape(local_queries, HEADS, per_head)
    grad_three = attn_grad.reshape(local_queries, HEADS, per_head)
    logit_grad = (
        (attn_three * (grad_three - jnp.sum(attn_three * grad_three, axis=2, keepdims=True)))
        .reshape(local_queries, att_width)
        .astype(jnp.bfloat16)
    )
    query_grad = times_transpose(logit_grad, attn_weight).astype(jnp.bfloat16)
    feature_grad = times_transpose(value_rounded, value_weight).astype(jnp.bfloat16)
    summed = sum_everywhere(shares[:, : terms.shape[1]])
    return (
        feature_grad[None],
        query_grad[None],
        summed[:, :width],
        summed[:, width : width + att_width],
        summed[:, width + att_width :],
    )


def solution(mesh):
    in_specs = (
        P("dp", ("tile", "query"), None),
        P("dp", ("tile", "query"), None),
        P("dp", ("tile", "query"), None),
        P(),
        P(),
        P(),
        P("dp", ("tile", "query")),
        P("dp", None, ("tile", "query")),
        P("dp", None, ("tile", "query")),
        P("dp", ("tile", "query")),
    )
    out_specs = (P("dp", ("tile", "query"), None), P("dp", ("tile", "query"), None), P(), P(), P())
    return jax.shard_map(local, mesh=mesh, in_specs=in_specs, out_specs=out_specs, check_vma=False)
```

```python
import jax
import jax.numpy as jnp
from jax import lax
from jax.experimental.layout import Layout, with_layout_constraint
from jax.sharding import PartitionSpec as P

HEADS = 8
TILE_W = 64


def over_rows(left, right):
    return lax.dot_general(
        left, right, (((0,), (0,)), ((), ())), preferred_element_type=jnp.float32
    )


def over_rows_exact(left, right):
    return lax.dot_general(
        left,
        right,
        (((0,), (0,)), ((), ())),
        precision=lax.Precision.HIGHEST,
        preferred_element_type=jnp.float32,
    )


def times_transpose(left, right):
    return lax.dot_general(
        left, right, (((1,), (1,)), ((), ())), preferred_element_type=jnp.float32
    )


def gather_rows(block, axes):
    count = lax.axis_size(axes)
    copies = jnp.broadcast_to(block[None], (count,) + block.shape)
    gathered = lax.all_to_all(copies, axes, 0, 0, tiled=True)
    return gathered.reshape((count * block.shape[0],) + block.shape[1:])


def scatter_sum_rows(block, axes):
    count = lax.axis_size(axes)
    pieces = block.reshape((count, block.shape[0] // count) + block.shape[1:])
    return jnp.sum(lax.all_to_all(pieces, axes, 0, 0, tiled=True), axis=0)


def sum_everywhere(block):
    count = lax.axis_size("dp")
    copies = jnp.broadcast_to(block[None], (count,) + block.shape)
    block = jnp.sum(lax.all_to_all(copies, "dp", 0, 0, tiled=True), axis=0)
    return gather_rows(block, ("tile", "query"))

def row_major(block):
    return with_layout_constraint(block, Layout(major_to_minor=(0, 1)))


def shift_down(block, offset):
    return jnp.concatenate(
        [jnp.zeros((offset, block.shape[1]), block.dtype), block[: block.shape[0] - offset]], axis=0
    )


def local(
    features,
    queries,
    out_grad,
    value_weight,
    attn_weight,
    out_weight,
    slot_point,
    slot_rows,
    slot_bilinear,
    slot_count,
):
    owners = lax.axis_size(("tile", "query"))
    page_count = lax.axis_size("dp")
    local_queries = queries.shape[1]
    all_queries = local_queries * owners
    grad_scale = float(page_count * all_queries) ** (-0.5)
    width = features.shape[2]
    att_width = attn_weight.shape[1]
    per_head = att_width // HEADS
    head_width = width // HEADS
    exponent = jnp.exp(
        jnp.dot(queries[0], attn_weight, preferred_element_type=jnp.float32)
    ).reshape(local_queries, HEADS, per_head)
    attention = (exponent / jnp.sum(exponent, axis=2, keepdims=True)).reshape(
        local_queries, att_width
    )
    sample_grad = times_transpose(out_grad[0], out_weight).astype(jnp.bfloat16)
    every_both = gather_rows(
        jnp.concatenate([sample_grad, out_grad[0], queries[0]], axis=1), ("tile", "query")
    )
    every_grad = every_both[:, :width]
    every_out = every_both[:, width : 2 * width]
    every_queries = every_both[:, 2 * width :]
    page_exponent = jnp.exp(
        jnp.dot(every_queries, attn_weight, preferred_element_type=jnp.float32)
    ).reshape(all_queries, HEADS, per_head)
    page_attention = page_exponent / jnp.sum(page_exponent, axis=2, keepdims=True)
    every_attn = page_attention.reshape(all_queries, att_width).astype(jnp.bfloat16)
    projected = jnp.dot(features[0], value_weight, preferred_element_type=jnp.float32).astype(
        jnp.bfloat16
    )
    token_count = projected.shape[0]
    capacity = slot_point.shape[1]
    points = slot_point[0]
    alive_slot = jnp.arange(capacity, dtype=jnp.int32) < slot_count[0, 0]
    query_index = points // att_width
    attn_column = points % att_width
    head_index = attn_column // per_head
    query_match = query_index[:, None] == jnp.arange(all_queries, dtype=jnp.int32)[None, :]
    query_onehot = query_match.astype(jnp.bfloat16)
    column_match = attn_column[:, None] == jnp.arange(att_width, dtype=jnp.int32)[None, :]
    picked_rows = jnp.dot(
        query_onehot,
        jnp.concatenate([every_grad, every_attn], axis=1),
        preferred_element_type=jnp.float32,
    )
    grad_rows = picked_rows[:, :width]
    attn_rows = picked_rows[:, width:]
    picked_attn = jnp.sum(jnp.where(column_match, attn_rows, jnp.zeros((), jnp.float32)), axis=1)
    weight = jnp.where(alive_slot, picked_attn, jnp.zeros((), jnp.float32))
    head_mask = jnp.arange(width, dtype=jnp.int32)[None, :] // head_width == head_index[:, None]
    slot_grad = row_major(jnp.where(head_mask, grad_rows, jnp.zeros((), jnp.float32)))
    offsets = (0, 1, TILE_W, TILE_W + 1)
    padded = jnp.concatenate([projected, jnp.zeros((TILE_W + 1, width), jnp.bfloat16)], axis=0)
    corner_table = jnp.concatenate(
        [padded[offset : offset + token_count] for offset in offsets], axis=1
    )
    base_row = slot_rows[0, 0]
    picked_all = row_major(corner_table[base_row])
    mixed_rows = jnp.zeros((capacity, width), jnp.float32)
    contributions = []
    for corner in range(4):
        bilinear = slot_bilinear[0, corner]
        picked = picked_all[:, corner * width : (corner + 1) * width].astype(jnp.float32)
        mixed_rows = mixed_rows + bilinear[:, None] * picked
        contributions.append((weight * bilinear)[:, None] * slot_grad)
    corner_dots = jnp.sum(mixed_rows * slot_grad, axis=1)
    margin = TILE_W + 1
    corner_sums = (
        jnp.zeros((token_count + margin, 4 * width), jnp.float32)
        .at[base_row + margin]
        .add(row_major(jnp.concatenate(contributions, axis=1)))
    )
    value_grad = corner_sums[margin : margin + token_count, 0:width]
    for corner in range(1, 4):
        start = margin - offsets[corner]
        value_grad = (
            value_grad
            + corner_sums[start : start + token_count, corner * width : (corner + 1) * width]
        )
    value_rounded = value_grad.astype(jnp.bfloat16)
    value_term = over_rows(features[0], value_rounded)
    query_float = query_match.astype(jnp.float32)
    sampled_part = over_rows_exact(
        query_float, jnp.where(head_mask, weight[:, None] * mixed_rows, jnp.zeros((), jnp.float32))
    )
    dots_table = jnp.where(
        jnp.logical_and(column_match, alive_slot[:, None]),
        corner_dots[:, None],
        jnp.zeros((), jnp.float32),
    )
    attn_part = over_rows_exact(query_float, dots_table)
    out_term = over_rows_exact(sampled_part, every_out.astype(jnp.float32))
    part_three = attn_part.reshape(all_queries, HEADS, per_head)
    part_logits = (
        page_attention
        * (part_three - jnp.sum(page_attention * part_three, axis=2, keepdims=True))
    ).reshape(all_queries, att_width)
    attn_term = over_rows_exact(every_queries.astype(jnp.float32), part_logits)
    terms = jnp.concatenate([value_term, attn_term, out_term], axis=1) * grad_scale
    shares = scatter_sum_rows(jnp.concatenate([terms, attn_part], axis=1), ("tile", "query"))
    attn_grad = shares[:, terms.shape[1] :]
    attn_three = attention.reshape(local_queries, HEADS, per_head)
    grad_three = attn_grad.reshape(local_queries, HEADS, per_head)
    logit_grad = (
        (attn_three * (grad_three - jnp.sum(attn_three * grad_three, axis=2, keepdims=True)))
        .reshape(local_queries, att_width)
        .astype(jnp.bfloat16)
    )
    query_grad = times_transpose(logit_grad, attn_weight).astype(jnp.bfloat16)
    feature_grad = times_transpose(value_rounded, value_weight).astype(jnp.bfloat16)
    summed = sum_everywhere(shares[:, : terms.shape[1]])
    return (
        feature_grad[None],
        query_grad[None],
        summed[:, :width],
        summed[:, width : width + att_width],
        summed[:, width + att_width :],
    )


def solution(mesh):
    in_specs = (
        P("dp", ("tile", "query"), None),
        P("dp", ("tile", "query"), None),
        P("dp", ("tile", "query"), None),
        P(),
        P(),
        P(),
        P("dp", ("tile", "query")),
        P("dp", None, ("tile", "query")),
        P("dp", None, ("tile", "query")),
        P("dp", ("tile", "query")),
    )
    out_specs = (P("dp", ("tile", "query"), None), P("dp", ("tile", "query"), None), P(), P(), P())
    return jax.shard_map(local, mesh=mesh, in_specs=in_specs, out_specs=out_specs, check_vma=False)
```
